32 devices in a mesh: groups: 2 (over y), ctx: 8 (over z, x), ch: 2 (over core).
Axes of the slice: x: 2, y: 2, z: 4, core: 2. Of those that a mesh axis runs over, the one named last changes fastest.
Arguments:
- gate_stream: bfloat16 [4096, 512], P(('groups', 'ctx'), 'ch'), parts along dimension 0, may hold values from -6 to 6
- outer_stream: bfloat16 [4096, 512], P(('groups', 'ctx'), 'ch'), parts along dimension 0, may hold values from -6 to 6
- value_stream: bfloat16 [4096, 512], P(('groups', 'ctx'), 'ch'), parts along dimension 0, may hold values from -6 to 6
- short_weight: bfloat16 [3, 3, 512], P(None, None, 'ch'), may hold values from -3.5 to 3.5
- long_filter: bfloat16 [2048, 512], P('ctx', 'ch'), may hold values from -0.125 to 0.125
- skip_gain: float32 [512], P('ch'), may hold values from -4 to 4
Outputs:
- output_rows: bfloat16 [4096, 512], P(('groups', 'ctx'), 'ch'), parts along dimension 0
The draws below stay inside these ranges and needn't reach their ends.
There are 2 independent parts, one for each index of `groups`. The reference program is written for one: setup_inputs(seed, part) draws one part's arguments, and reference() takes and returns one part's arrays. A program takes and returns all parts, laid end to end along the dimension named above; an argument that names none is the same for every part. Nothing has to cross between parts.
All inputs are finite; a program needn't handle non-finite values.
Results may differ from the reference program's by a relative error of at most 0.001.
Values may be sent and summed in bfloat16 or wider, within the bound.
No kernel may reach another device: no remote copies, remote signals or barrier semaphores. Data moves between devices by JAX's collectives and lax.ppermute only.
A program may use at most 64 MiB of HBM per device.

```python
import jax
import jax.numpy as jnp

CH = 512
TAPS = 3
SEQ = 2048


def block_levels(key, dims, cuts, smallest, top_value):
    def one(dim, shards_of):
        draws = jax.random.uniform(jax.random.fold_in(jax.random.fold_in(key, 6), dim), (shards_of,), jnp.float32, smallest / len(cuts), top_value / len(cuts))
        return jnp.repeat(jnp.exp(draws), dims[dim] // shards_of).reshape((-1,) + (1,) * (len(dims) - dim - 1))

    gain = one(*cuts[0])
    for cut in cuts[1:]:
        gain = gain * one(*cut)
    return gain


def normal_values(stream_key, shape, width, bound, shards=(), kind=jnp.bfloat16):
    result = jax.random.normal(stream_key, shape, jnp.float32) * width
    if len(shards) > 0:
        result = block_levels(stream_key, shape, shards, -0.22, 0.18) * result
    return jnp.clip(result, min=-bound, max=bound).astype(kind)


def setup_inputs(seed: int = 0, part: int = 0) -> dict:
    arg_keys = jax.random.split(jax.random.key(seed), 7)
    part_splits = jax.random.split(jax.random.fold_in(arg_keys[6], part), 7)
    gate_stream = normal_values(part_splits[0], (SEQ, CH), 1.0, 6.0, ((0, 8), (1, 2)))
    outer_stream = normal_values(part_splits[1], (SEQ, CH), 1.0, 6.0, ((0, 8), (1, 2)))
    value_stream = normal_values(part_splits[2], (SEQ, CH), 1.0, 6.0, ((0, 8), (1, 2)))
    short_weight = normal_values(arg_keys[3], (3, TAPS, CH), TAPS ** -0.5, 3.5, ((2, 2),))
    long_filter = normal_values(arg_keys[4], (SEQ, CH), SEQ ** -0.5, 0.125, ((0, 8), (1, 2)))
    skip_gain = normal_values(arg_keys[5], (CH,), 1.0, 4.0, ((0, 2),), jnp.float32)
    return {"gate_stream": gate_stream, "outer_stream": outer_stream, "value_stream": value_stream, "short_weight": short_weight, "long_filter": long_filter, "skip_gain": skip_gain}


def short_conv(stream, kernel):
    padded = jnp.pad(stream.astype(jnp.float32), ((TAPS - 1, 0), (0, 0)))
    summed = jnp.zeros(stream.shape, jnp.float32)
    for offset in range(TAPS):
        begin_at = TAPS - 1 - offset
        summed = summed + kernel[offset].astype(jnp.float32) * padded[begin_at:begin_at + SEQ]
    return summed


def reference(gate_stream, outer_stream, value_stream, short_weight, long_filter, skip_gain):
    gate_conv = short_conv(gate_stream, short_weight[0])
    outer_conv = short_conv(outer_stream, short_weight[1])
    value_conv = short_conv(value_stream, short_weight[2])
    gated_value = gate_conv * value_conv
    spectrum = jnp.fft.rfft(gated_value, n=2 * SEQ, axis=0) * jnp.fft.rfft(long_filter.astype(jnp.float32), n=2 * SEQ, axis=0)
    long_part = jnp.fft.irfft(spectrum, n=2 * SEQ, axis=0)[:SEQ]
    output_rows = outer_conv * (long_part + skip_gain[None, :] * gated_value)
    return output_rows.astype(jnp.bfloat16)
```

```python
import math

import numpy as np

import jax
import jax.numpy as jnp
from jax import lax
from jax.sharding import PartitionSpec as P

full_precision = lax.Precision.HIGHEST


def transform_tables(blocks, rows):
    total = 2 * blocks * rows
    k2 = np.arange(blocks + 1)
    d = np.arange(blocks)
    r = np.arange(rows)
    block_angle = 2.0 * np.pi * np.outer(k2, d) / (2 * blocks)
    first = np.concatenate([np.cos(block_angle), -np.sin(block_angle)], axis=0)
    twist_angle = -2.0 * np.pi * np.outer(k2, r) / total
    twist = np.stack([np.cos(twist_angle), np.sin(twist_angle)])
    row_angle = 2.0 * np.pi * np.outer(r, r) / rows
    cosine, sine = np.cos(row_angle), np.sin(row_angle)
    forward = np.block([[cosine, -sine], [sine, cosine]])
    backward = np.block([[cosine, sine], [-sine, cosine]])
    weight = np.full(blocks + 1, 2.0)
    weight[0] = 1.0
    weight[-1] = 1.0
    last_angle = 2.0 * np.pi * np.outer(d, k2) / (2 * blocks)
    last = np.concatenate(
        [weight * np.cos(last_angle), -weight * np.sin(last_angle)], axis=1
    ) / total
    as_f32 = lambda a: jnp.asarray(a.astype(np.float32))
    return tuple(as_f32(a) for a in (first, twist, forward, backward, last))


def shifted(x, lag):
    if lag == 0:
        return x
    earlier = jnp.concatenate([jnp.zeros_like(x[:1]), x[:-1]], axis=0)
    return jnp.concatenate([earlier[:, :, -lag:], x[:, :, :-lag]], axis=2)


def short_conv(x, kernel):
    summed = kernel[0][None, :, None] * x
    for lag in range(1, kernel.shape[0]):
        summed = summed + kernel[lag][None, :, None] * shifted(x, lag)
    return summed


def complex_rows(re, im, table):
    both = jnp.concatenate([re, im], axis=-1)
    out = jnp.einsum("...j,jk->...k", both, table, precision=full_precision)
    half = out.shape[-1] // 2
    return out[..., :half], out[..., half:]


def body(gate_stream, outer_stream, value_stream, short_weight, long_filter, skip_gain):
    rows, chans = gate_stream.shape
    blocks = lax.axis_size("ctx")
    piece = chans // blocks
    me = lax.axis_index("ctx")
    first, twist, forward, backward, last = transform_tables(blocks, rows)

    stacked = jnp.stack([gate_stream, value_stream, outer_stream, long_filter])
    stacked = jnp.swapaxes(stacked, 1, 2).reshape(4, blocks, piece, rows)
    gathered = lax.all_to_all(stacked, "ctx", 1, 1)
    signals = gathered.astype(jnp.float32)

    kernels = lax.dynamic_slice_in_dim(short_weight, me * piece, piece, axis=2).astype(jnp.float32)
    gain = lax.dynamic_slice_in_dim(skip_gain, me * piece, piece)

    gate_conv = short_conv(signals[0], kernels[0])
    value_conv = short_conv(signals[1], kernels[2])
    outer_conv = short_conv(signals[2], kernels[1])
    gated_value = gate_conv * value_conv

    pair = jnp.stack([gated_value, signals[3]])
    spread = jnp.einsum("kd,sdcr->skcr", first, pair, precision=full_precision)
    half = blocks + 1
    a_re, a_im = spread[:, :half], spread[:, half:]
    t_re = twist[0][None, :, None, :]
    t_im = twist[1][None, :, None, :]
    b_re = a_re * t_re - a_im * t_im
    b_im = a_re * t_im + a_im * t_re
    x_re, x_im = complex_rows(b_re, b_im, forward)
    q_re = x_re[0] * x_re[1] - x_im[0] * x_im[1]
    q_im = x_re[0] * x_im[1] + x_im[0] * x_re[1]
    y_re, y_im = complex_rows(q_re, q_im, backward)
    u_re = y_re * twist[0][:, None, :] + y_im * twist[1][:, None, :]
    u_im = y_im * twist[0][:, None, :] - y_re * twist[1][:, None, :]
    long_part = jnp.einsum(
        "dk,kcr->dcr", last, jnp.concatenate([u_re, u_im], axis=0), precision=full_precision
    )

    out = outer_conv * (long_part + gain[None, :, None] * gated_value)
    out = out.astype(jnp.bfloat16)
    returned = lax.all_to_all(out, "ctx", 0, 0)
    return jnp.swapaxes(returned.reshape(chans, rows), 0, 1)


def solution(mesh):
    placed = (
        P(("groups", "ctx"), "ch"),
        P(("groups", "ctx"), "ch"),
        P(("groups", "ctx"), "ch"),
        P(None, None, "ch"),
        P("ctx", "ch"),
        P("ch"),
    )
    return jax.shard_map(
        body, mesh=mesh, in_specs=placed, out_specs=P(("groups", "ctx"), "ch"), check_vma=False
    )
```

```python
import math

import numpy as np

import jax
import jax.numpy as jnp
from jax import lax
from jax.sharding import PartitionSpec as P

full_precision = lax.Precision.HIGHEST


def transform_tables(blocks, rows):
    total = 2 * blocks * rows
    k2 = np.arange(blocks + 1)
    d = np.arange(blocks)
    r = np.arange(rows)
    block_angle = 2.0 * np.pi * np.outer(k2, d) / (2 * blocks)
    first = np.concatenate([np.cos(block_angle), -np.sin(block_angle)], axis=0)
    twist_angle = -2.0 * np.pi * np.outer(k2, r) / total
    twist = np.stack([np.cos(twist_angle), np.sin(twist_angle)])
    row_angle = 2.0 * np.pi * np.outer(r, r) / rows
    cosine, sine = np.cos(row_angle), np.sin(row_angle)
    forward = np.block([[cosine, -sine], [sine, cosine]])
    backward = np.block([[cosine, sine], [-sine, cosine]])
    weight = np.full(blocks + 1, 2.0)
    weight[0] = 1.0
    weight[-1] = 1.0
    last_angle = 2.0 * np.pi * np.outer(d, k2) / (2 * blocks)
    last = np.concatenate(
        [weight * np.cos(last_angle), -weight * np.sin(last_angle)], axis=1
    ) / total
    as_f32 = lambda a: jnp.asarray(a.astype(np.float32))
    return tuple(as_f32(a) for a in (first, twist, forward, backward, last))


def shifted(x, lag):
    if lag == 0:
        return x
    earlier = jnp.concatenate([jnp.zeros_like(x[:1]), x[:-1]], axis=0)
    return jnp.concatenate([earlier[:, :, -lag:], x[:, :, :-lag]], axis=2)


def short_conv(x, kernel):
    summed = kernel[0][None, :, None] * x
    for lag in range(1, kernel.shape[0]):
        summed = summed + kernel[lag][None, :, None] * shifted(x, lag)
    return summed


def complex_rows(re, im, table):
    both = jnp.concatenate([re, im], axis=-1)
    out = jnp.einsum("...j,jk->...k", both, table, precision=full_precision)
    half = out.shape[-1] // 2
    return out[..., :half], out[..., half:]


def exchange(x, count, me, axis):
    received = [lax.index_in_dim(lax.dynamic_slice_in_dim(x, me, 1, axis), 0, axis, keepdims=False)]
    for distance in range(1, count):
        pairs = [(i, (i + distance) % count) for i in range(count)]
        part = lax.dynamic_slice_in_dim(x, (me + distance) % count, 1, axis)
        received.append(lax.index_in_dim(lax.ppermute(part, "ctx", pairs), 0, axis, keepdims=False))
    by_distance = jnp.stack(received, axis=axis)
    order = (me - jnp.arange(count, dtype=jnp.int32)) % count
    return jnp.take(by_distance, order, axis=axis)


def body(gate_stream, outer_stream, value_stream, short_weight, long_filter, skip_gain):
    rows, chans = gate_stream.shape
    blocks = lax.axis_size("ctx")
    piece = chans // blocks
    me = lax.axis_index("ctx")
    first, twist, forward, backward, last = transform_tables(blocks, rows)

    stacked = jnp.stack([gate_stream, value_stream, outer_stream, long_filter])
    stacked = jnp.swapaxes(stacked, 1, 2).reshape(4, blocks, piece, rows)
    gathered = exchange(stacked, blocks, me, 1)
    signals = gathered.astype(jnp.float32)

    kernels = lax.dynamic_slice_in_dim(short_weight, me * piece, piece, axis=2).astype(jnp.float32)
    gain = lax.dynamic_slice_in_dim(skip_gain, me * piece, piece)

    gate_conv = short_conv(signals[0], kernels[0])
    value_conv = short_conv(signals[1], kernels[2])
    outer_conv = short_conv(signals[2], kernels[1])
    gated_value = gate_conv * value_conv

    pair = jnp.stack([gated_value, signals[3]])
    spread = jnp.einsum("kd,sdcr->skcr", first, pair, precision=full_precision)
    half = blocks + 1
    a_re, a_im = spread[:, :half], spread[:, half:]
    t_re = twist[0][None, :, None, :]
    t_im = twist[1][None, :, None, :]
    b_re = a_re * t_re - a_im * t_im
    b_im = a_re * t_im + a_im * t_re
    x_re, x_im = complex_rows(b_re, b_im, forward)
    q_re = x_re[0] * x_re[1] - x_im[0] * x_im[1]
    q_im = x_re[0] * x_im[1] + x_im[0] * x_re[1]
    y_re, y_im = complex_rows(q_re, q_im, backward)
    u_re = y_re * twist[0][:, None, :] + y_im * twist[1][:, None, :]
    u_im = y_im * twist[0][:, None, :] - y_re * twist[1][:, None, :]
    long_part = jnp.einsum(
        "dk,kcr->dcr", last, jnp.concatenate([u_re, u_im], axis=0), precision=full_precision
    )

    out = outer_conv * (long_part + gain[None, :, None] * gated_value)
    out = out.astype(jnp.bfloat16)
    returned = exchange(out, blocks, me, 0)
    return jnp.swapaxes(returned.reshape(chans, rows), 0, 1)


def solution(mesh):
    placed = (
        P(("groups", "ctx"), "ch"),
        P(("groups", "ctx"), "ch"),
        P(("groups", "ctx"), "ch"),
        P(None, None, "ch"),
        P("ctx", "ch"),
        P("ch"),
    )
    return jax.shard_map(
        body, mesh=mesh, in_specs=placed, out_specs=P(("groups", "ctx"), "ch"), check_vma=False
    )
```

```python
import math

import ml_dtypes
import numpy as np

import jax
import jax.numpy as jnp
from jax import lax
from jax.experimental import pallas as pl
from jax.experimental.pallas import tpu as pltpu
from jax.sharding import PartitionSpec as P

full_precision = lax.Precision.HIGHEST


def split_table(table):
    high = table.astype(ml_dtypes.bfloat16)
    low = (table - high.astype(np.float64)).astype(ml_dtypes.bfloat16)
    return jnp.asarray(high), jnp.asarray(low)


def kernel_tables(blocks, rows, piece):
    total = 2 * blocks * rows
    half = blocks + 1
    k2 = np.arange(half)
    d = np.arange(blocks)
    r = np.arange(rows)
    clean = lambda a: np.where(np.abs(a) < 1e-12, 0.0, a)
    block_angle = 2.0 * np.pi * np.outer(k2, d) / (2 * blocks)
    first = clean(np.concatenate([np.cos(block_angle), -np.sin(block_angle)], axis=0))
    twist_angle = -2.0 * np.pi * np.outer(k2, r) / total
    twist = np.stack([np.cos(twist_angle), np.sin(twist_angle)])
    twist = np.repeat(twist, piece, axis=1)
    row_angle = 2.0 * np.pi * np.outer(r, r) / rows
    cosine, sine = np.cos(row_angle), np.sin(row_angle)
    forward = np.block([[cosine, -sine], [sine, cosine]])
    backward = np.block([[cosine, sine], [-sine, cosine]])
    weight = np.full(half, 2.0)
    weight[0] = 1.0
    weight[-1] = 1.0
    last_angle = 2.0 * np.pi * np.outer(d, k2) / (2 * blocks)
    last = clean(np.concatenate([weight * np.cos(last_angle), -weight * np.sin(last_angle)], axis=1))
    last = last / total
    as_f32 = lambda a: jnp.asarray(a.astype(np.float32))
    return (as_f32(first), as_f32(last), as_f32(twist)) + split_table(forward) + split_table(backward)


def dot3(a, high_ref, low_ref):
    a_high = a.astype(jnp.bfloat16)
    a_low = (a - a_high.astype(jnp.float32)).astype(jnp.bfloat16)
    high = high_ref[...]
    out = jnp.dot(a_high, high, preferred_element_type=jnp.float32)
    out = out + jnp.dot(a_low, high, preferred_element_type=jnp.float32)
    return out + jnp.dot(a_high, low_ref[...], preferred_element_type=jnp.float32)


def local_kernel(first, last, sig, kern, gain, twist, fwd_hi, fwd_lo, bwd_hi, bwd_lo, out,
                 ext, g_s, o_s, a_g, a_h):
    blocks, piece, rows = out.shape
    half = blocks + 1
    taps = kern.shape[1]
    tile = min(piece, 8)
    unrolled = blocks <= 16
    f32 = jnp.float32
    lane = lax.broadcasted_iota(jnp.int32, (blocks, piece, rows), 2)
    ext[0] = jnp.zeros((piece, rows), f32)

    def conv(stream, weights):
        x = sig[stream].astype(f32)
        total = kern[weights, 0] * x
        for lag in range(1, taps):
            rolled = pltpu.roll(x, lag, 2)
            ext[pl.ds(1, blocks)] = rolled
            earlier = jnp.where(lane < lag, ext[pl.ds(0, blocks)], rolled)
            total = total + kern[weights, lag] * earlier
        return total

    g_s[...] = conv(0, 0) * conv(1, 2)
    o_s[...] = conv(2, 1)

    def load_block(which, d, at):
        if which == 0:
            return g_s[d, at, :]
        return sig[3, d, at, :].astype(f32)

    for tile_index in range(piece // tile):
        at = pl.ds(tile_index * tile, tile)
        for which, dst in ((0, a_g), (1, a_h)):
            if unrolled:
                xs = [load_block(which, d, at) for d in range(blocks)]
                for k in range(half):
                    for part in range(2):
                        acc = first[part * half + k, 0] * xs[0]
                        for d in range(1, blocks):
                            acc = acc + first[part * half + k, d] * xs[d]
                        dst[pl.ds(k * piece + tile_index * tile, tile), pl.ds(part * rows, rows)] = acc
            else:
                for k in range(half):
                    for part in range(2):
                        dst[pl.ds(k * piece + tile_index * tile, tile), pl.ds(part * rows, rows)] = (
                            jnp.zeros((tile, rows), f32))

                def step(d, carry):
                    xd = load_block(which, d, at)
                    for k in range(half):
                        for part in range(2):
                            where = (pl.ds(k * piece + tile_index * tile, tile), pl.ds(part * rows, rows))
                            dst[where] = dst[where] + first[part * half + k, d] * xd
                    return carry

                lax.fori_loop(0, blocks, step, 0)

    t_re = twist[0]
    t_im = twist[1]
    spectra = []
    for src in (a_g, a_h):
        re = src[:, pl.ds(0, rows)]
        im = src[:, pl.ds(rows, rows)]
        turned = jnp.concatenate([re * t_re - im * t_im, re * t_im + im * t_re], axis=1)
        spectra.append(dot3(turned, fwd_hi, fwd_lo))
    xg, xh = spectra
    gr, gi = xg[:, :rows], xg[:, rows:]
    hr, hi = xh[:, :rows], xh[:, rows:]
    product = jnp.concatenate([gr * hr - gi * hi, gr * hi + gi * hr], axis=1)
    back = dot3(product, bwd_hi, bwd_lo)
    y_re, y_im = back[:, :rows], back[:, rows:]
    a_h[:, pl.ds(0, rows)] = y_re * t_re + y_im * t_im
    a_h[:, pl.ds(rows, rows)] = y_im * t_re - y_re * t_im

    for tile_index in range(piece // tile):
        at = pl.ds(tile_index * tile, tile)
        scale = gain[at]

        def finish(d, us):
            acc = None
            for k in range(half):
                for part in range(2):
                    term = last[d, part * half + k] * us(k, part)
                    acc = term if acc is None else acc + term
            gated = g_s[d, at, :]
            out[d, at, :] = (o_s[d, at, :] * (acc + scale * gated)).astype(out.dtype)

        if unrolled:
            held = {}
            for k in range(half):
                for part in range(2):
                    held[k, part] = a_h[pl.ds(k * piece + tile_index * tile, tile), pl.ds(part * rows, rows)]
            for d in range(blocks):
                finish(d, lambda k, part: held[k, part])
        else:
            def step(d, carry):
                finish(d, lambda k, part: a_h[
                    pl.ds(k * piece + tile_index * tile, tile), pl.ds(part * rows, rows)])
                return carry

            lax.fori_loop(0, blocks, step, 0)


def body(gate_stream, outer_stream, value_stream, short_weight, long_filter, skip_gain):
    rows, chans = gate_stream.shape
    blocks = lax.axis_size("ctx")
    piece = chans // blocks
    half = blocks + 1
    me = lax.axis_index("ctx")
    first, last, twist, fwd_hi, fwd_lo, bwd_hi, bwd_lo = kernel_tables(blocks, rows, piece)

    stacked = jnp.stack([gate_stream, value_stream, outer_stream, long_filter])
    stacked = jnp.swapaxes(stacked, 1, 2).reshape(4, blocks, piece, rows)
    gathered = lax.all_to_all(stacked, "ctx", 1, 1)

    kern = lax.dynamic_slice_in_dim(short_weight, me * piece, piece, axis=2).astype(jnp.float32)
    kern = kern[..., None]
    gain = lax.dynamic_slice_in_dim(skip_gain, me * piece, piece)[:, None]

    smem = pl.BlockSpec(memory_space=pltpu.SMEM)
    vmem = pl.BlockSpec(memory_space=pltpu.VMEM)
    f32 = jnp.float32
    out = pl.pallas_call(
        local_kernel,
        out_shape=jax.ShapeDtypeStruct((blocks, piece, rows), jnp.bfloat16),
        in_specs=[smem, smem] + [vmem] * 8,
        out_specs=vmem,
        scratch_shapes=[
            pltpu.VMEM((blocks + 1, piece, rows), f32),
            pltpu.VMEM((blocks, piece, rows), f32),
            pltpu.VMEM((blocks, piece, rows), f32),
            pltpu.VMEM((half * piece, 2 * rows), f32),
            pltpu.VMEM((half * piece, 2 * rows), f32),
        ],
    )(first, last, gathered, kern, gain, twist, fwd_hi, fwd_lo, bwd_hi, bwd_lo)

    returned = lax.all_to_all(out, "ctx", 0, 0)
    return jnp.swapaxes(returned.reshape(chans, rows), 0, 1)


def solution(mesh):
    placed = (
        P(("groups", "ctx"), "ch"),
        P(("groups", "ctx"), "ch"),
        P(("groups", "ctx"), "ch"),
        P(None, None, "ch"),
        P("ctx", "ch"),
        P("ch"),
    )
    return jax.shard_map(
        body, mesh=mesh, in_specs=placed, out_specs=P(("groups", "ctx"), "ch"), check_vma=False
    )
```

```python
import math

import ml_dtypes
import numpy as np

import jax
import jax.numpy as jnp
from jax import lax
from jax.experimental import pallas as pl
from jax.experimental.pallas import tpu as pltpu
from jax.sharding import PartitionSpec as P

full_precision = lax.Precision.HIGHEST


def split_table(table):
    high = table.astype(ml_dtypes.bfloat16)
    low = (table - high.astype(np.float64)).astype(ml_dtypes.bfloat16)
    return jnp.asarray(high), jnp.asarray(low)


def kernel_tables(blocks, rows, piece):
    total = 2 * blocks * rows
    half = blocks + 1
    k2 = np.arange(half)
    d = np.arange(blocks)
    r = np.arange(rows)
    clean = lambda a: np.where(np.abs(a) < 1e-12, 0.0, a)
    block_angle = 2.0 * np.pi * np.outer(k2, d) / (2 * blocks)
    first = clean(np.concatenate([np.cos(block_angle), -np.sin(block_angle)], axis=0))
    twist_angle = -2.0 * np.pi * np.outer(k2, r) / total
    twist = np.stack([np.cos(twist_angle), np.sin(twist_angle)])
    twist = np.repeat(twist, piece, axis=1)
    row_angle = 2.0 * np.pi * np.outer(r, r) / rows
    cosine, sine = np.cos(row_angle), np.sin(row_angle)
    forward = np.block([[cosine, -sine], [sine, cosine]])
    backward = np.block([[cosine, sine], [-sine, cosine]])
    weight = np.full(half, 2.0)
    weight[0] = 1.0
    weight[-1] = 1.0
    last_angle = 2.0 * np.pi * np.outer(d, k2) / (2 * blocks)
    last = clean(np.concatenate([weight * np.cos(last_angle), -weight * np.sin(last_angle)], axis=1))
    last = last / total
    as_f32 = lambda a: jnp.asarray(a.astype(np.float32))
    return (as_f32(first), as_f32(last), as_f32(twist)) + split_table(forward) + split_table(backward)


def dot3(a, high_ref, low_ref):
    a_high = a.astype(jnp.bfloat16)
    a_low = (a - a_high.astype(jnp.float32)).astype(jnp.bfloat16)
    high = high_ref[...]
    out = jnp.dot(a_high, high, preferred_element_type=jnp.float32)
    out = out + jnp.dot(a_low, high, preferred_element_type=jnp.float32)
    return out + jnp.dot(a_high, low_ref[...], preferred_element_type=jnp.float32)


def local_kernel(first, last, sig, kern, gain, twist, fwd_hi, fwd_lo, bwd_hi, bwd_lo, out,
                 ext, g_s, o_s, a_g, a_h):
    blocks, piece, rows = out.shape
    half = blocks + 1
    taps = kern.shape[1]
    tile = min(piece, 8)
    unrolled = blocks <= 16
    f32 = jnp.float32
    lane = lax.broadcasted_iota(jnp.int32, (blocks, piece, rows), 2)
    ext[0] = jnp.zeros((piece, rows), f32)

    def conv(stream, weights):
        x = sig[:, stream].astype(f32)
        total = kern[weights, 0] * x
        for lag in range(1, taps):
            rolled = pltpu.roll(x, lag, 2)
            ext[pl.ds(1, blocks)] = rolled
            earlier = jnp.where(lane < lag, ext[pl.ds(0, blocks)], rolled)
            total = total + kern[weights, lag] * earlier
        return total

    g_s[...] = conv(0, 0) * conv(1, 2)
    o_s[...] = conv(2, 1)

    def load_block(which, d, at):
        if which == 0:
            return g_s[d, at, :]
        return sig[d, 3, at, :].astype(f32)

    for tile_index in range(piece // tile):
        at = pl.ds(tile_index * tile, tile)
        for which, dst in ((0, a_g), (1, a_h)):
            if unrolled:
                xs = [load_block(which, d, at) for d in range(blocks)]
                for k in range(half):
                    for part in range(2):
                        acc = first[part * half + k, 0] * xs[0]
                        for d in range(1, blocks):
                            acc = acc + first[part * half + k, d] * xs[d]
                        dst[pl.ds(k * piece + tile_index * tile, tile), pl.ds(part * rows, rows)] = acc
            else:
                for k in range(half):
                    for part in range(2):
                        dst[pl.ds(k * piece + tile_index * tile, tile), pl.ds(part * rows, rows)] = (
                            jnp.zeros((tile, rows), f32))

                def step(d, carry):
                    xd = load_block(which, d, at)
                    for k in range(half):
                        for part in range(2):
                            where = (pl.ds(k * piece + tile_index * tile, tile), pl.ds(part * rows, rows))
                            dst[where] = dst[where] + first[part * half + k, d] * xd
                    return carry

                lax.fori_loop(0, blocks, step, 0)

    t_re = twist[0]
    t_im = twist[1]
    spectra = []
    for src in (a_g, a_h):
        re = src[:, pl.ds(0, rows)]
        im = src[:, pl.ds(rows, rows)]
        turned = jnp.concatenate([re * t_re - im * t_im, re * t_im + im * t_re], axis=1)
        spectra.append(dot3(turned, fwd_hi, fwd_lo))
    xg, xh = spectra
    gr, gi = xg[:, :rows], xg[:, rows:]
    hr, hi = xh[:, :rows], xh[:, rows:]
    product = jnp.concatenate([gr * hr - gi * hi, gr * hi + gi * hr], axis=1)
    back = dot3(product, bwd_hi, bwd_lo)
    y_re, y_im = back[:, :rows], back[:, rows:]
    a_h[:, pl.ds(0, rows)] = y_re * t_re + y_im * t_im
    a_h[:, pl.ds(rows, rows)] = y_im * t_re - y_re * t_im

    for tile_index in range(piece // tile):
        at = pl.ds(tile_index * tile, tile)
        scale = gain[at]

        def finish(d, us):
            acc = None
            for k in range(half):
                for part in range(2):
                    term = last[d, part * half + k] * us(k, part)
                    acc = term if acc is None else acc + term
            gated = g_s[d, at, :]
            out[d, at, :] = (o_s[d, at, :] * (acc + scale * gated)).astype(out.dtype)

        if unrolled:
            held = {}
            for k in range(half):
                for part in range(2):
                    held[k, part] = a_h[pl.ds(k * piece + tile_index * tile, tile), pl.ds(part * rows, rows)]
            for d in range(blocks):
                finish(d, lambda k, part: held[k, part])
        else:
            def step(d, carry):
                finish(d, lambda k, part: a_h[
                    pl.ds(k * piece + tile_index * tile, tile), pl.ds(part * rows, rows)])
                return carry

            lax.fori_loop(0, blocks, step, 0)


def to_blocks_kernel(*refs):
    *streams, out, held = refs
    blocks, _, piece, rows = out.shape
    for index, stream in enumerate(streams):
        held[...] = jnp.transpose(stream[...].astype(jnp.float32))
        for j in range(blocks):
            out[j, index] = held[pl.ds(j * piece, piece), :].astype(out.dtype)


def from_blocks_kernel(pieces, out, held):
    blocks, piece, rows = pieces.shape
    for j in range(blocks):
        held[pl.ds(j * piece, piece), :] = pieces[j].astype(jnp.float32)
    out[...] = jnp.transpose(held[...]).astype(out.dtype)


def body(gate_stream, outer_stream, value_stream, short_weight, long_filter, skip_gain):
    rows, chans = gate_stream.shape
    blocks = lax.axis_size("ctx")
    piece = chans // blocks
    half = blocks + 1
    me = lax.axis_index("ctx")
    first, last, twist, fwd_hi, fwd_lo, bwd_hi, bwd_lo = kernel_tables(blocks, rows, piece)

    vmem = pl.BlockSpec(memory_space=pltpu.VMEM)
    stacked = pl.pallas_call(
        to_blocks_kernel,
        out_shape=jax.ShapeDtypeStruct((blocks, 4, piece, rows), jnp.bfloat16),
        in_specs=[vmem] * 4,
        out_specs=vmem,
        scratch_shapes=[pltpu.VMEM((chans, rows), jnp.float32)],
    )(gate_stream, value_stream, outer_stream, long_filter)
    gathered = lax.all_to_all(stacked, "ctx", 0, 0)

    kern = lax.dynamic_slice_in_dim(short_weight, me * piece, piece, axis=2).astype(jnp.float32)
    kern = kern[..., None]
    gain = lax.dynamic_slice_in_dim(skip_gain, me * piece, piece)[:, None]

    smem = pl.BlockSpec(memory_space=pltpu.SMEM)
    f32 = jnp.float32
    out = pl.pallas_call(
        local_kernel,
        out_shape=jax.ShapeDtypeStruct((blocks, piece, rows), jnp.bfloat16),
        in_specs=[smem, smem] + [vmem] * 8,
        out_specs=vmem,
        scratch_shapes=[
            pltpu.VMEM((blocks + 1, piece, rows), f32),
            pltpu.VMEM((blocks, piece, rows), f32),
            pltpu.VMEM((blocks, piece, rows), f32),
            pltpu.VMEM((half * piece, 2 * rows), f32),
            pltpu.VMEM((half * piece, 2 * rows), f32),
        ],
    )(first, last, gathered, kern, gain, twist, fwd_hi, fwd_lo, bwd_hi, bwd_lo)

    returned = lax.all_to_all(out, "ctx", 0, 0)
    return pl.pallas_call(
        from_blocks_kernel,
        out_shape=jax.ShapeDtypeStruct((rows, chans), jnp.bfloat16),
        in_specs=[vmem],
        out_specs=vmem,
        scratch_shapes=[pltpu.VMEM((chans, rows), jnp.float32)],
    )(returned)


def solution(mesh):
    placed = (
        P(("groups", "ctx"), "ch"),
        P(("groups", "ctx"), "ch"),
        P(("groups", "ctx"), "ch"),
        P(None, None, "ch"),
        P("ctx", "ch"),
        P("ch"),
    )
    return jax.shard_map(
        body, mesh=mesh, in_specs=placed, out_specs=P(("groups", "ctx"), "ch"), check_vma=False
    )
```

```python
import math

import ml_dtypes
import numpy as np

import jax
import jax.numpy as jnp
from jax import lax
from jax.experimental import pallas as pl
from jax.experimental.pallas import tpu as pltpu
from jax.sharding import PartitionSpec as P

full_precision = lax.Precision.HIGHEST


def split_table(table):
    high = table.astype(ml_dtypes.bfloat16)
    low = (table - high.astype(np.float64)).astype(ml_dtypes.bfloat16)
    return jnp.asarray(high), jnp.asarray(low)


def kernel_tables(blocks, rows):
    total = 2 * blocks * rows
    half = blocks + 1
    k2 = np.arange(half)
    d = np.arange(blocks)
    r = np.arange(rows)
    clean = lambda a: np.where(np.abs(a) < 1e-12, 0.0, a)
    block_angle = 2.0 * np.pi * np.outer(k2, d) / (2 * blocks)
    first = clean(np.concatenate([np.cos(block_angle), -np.sin(block_angle)], axis=0))
    twist_angle = -2.0 * np.pi * np.outer(k2, r) / total
    twist = np.stack([np.cos(twist_angle), np.sin(twist_angle)])[:, :, None, :]
    untwist = np.stack([np.cos(twist_angle), -np.sin(twist_angle)])[:, :, None, :] / total
    row_angle = 2.0 * np.pi * np.outer(r, r) / rows
    weight = np.full(half, 2.0)
    weight[0] = 1.0
    weight[-1] = 1.0
    last_angle = 2.0 * np.pi * np.outer(d, k2) / (2 * blocks)
    last = clean(np.concatenate([weight * np.cos(last_angle), -weight * np.sin(last_angle)], axis=1))
    as_f32 = lambda a: jnp.asarray(a.astype(np.float32))
    return ((as_f32(first), as_f32(last), as_f32(twist), as_f32(untwist))
            + split_table(np.cos(row_angle)) + split_table(np.sin(row_angle)))


def scaled(terms):
    total = None
    for array, constant in terms:
        if array is None or constant == 0.0:
            continue
        if constant == 1.0:
            term = array
        elif constant == -1.0:
            term = -array
        else:
            term = constant * array
        total = term if total is None else total + term
    return total


def unit(angle):
    c, s = math.cos(angle), math.sin(angle)
    snap = lambda v: 0.0 if abs(v) < 1e-12 else (1.0 if abs(v - 1) < 1e-12 else (-1.0 if abs(v + 1) < 1e-12 else v))
    return snap(c), snap(s)


def fft(values, sign):
    count = len(values)
    if count == 1:
        return values
    even = fft(values[0::2], sign)
    odd = fft(values[1::2], sign)
    out = [None] * count
    for k in range(count // 2):
        c, s = unit(sign * 2.0 * math.pi * k / count)
        o_re, o_im = odd[k]
        t_re = scaled([(o_re, c), (o_im, -s)])
        t_im = scaled([(o_re, s), (o_im, c)])
        e_re, e_im = even[k]
        out[k] = (scaled([(e_re, 1.0), (t_re, 1.0)]), scaled([(e_im, 1.0), (t_im, 1.0)]))
        out[k + count // 2] = (scaled([(e_re, 1.0), (t_re, -1.0)]), scaled([(e_im, 1.0), (t_im, -1.0)]))
    return out


def halves(a):
    high = a.astype(jnp.bfloat16)
    return high, (a - high.astype(jnp.float32)).astype(jnp.bfloat16)


def times(parts, high_ref, low_ref):
    high, low = parts
    table = high_ref[...]
    out = jnp.dot(high, table, preferred_element_type=jnp.float32)
    out = out + jnp.dot(low, table, preferred_element_type=jnp.float32)
    return out + jnp.dot(high, low_ref[...], preferred_element_type=jnp.float32)


def local_kernel(first, last, sig, kern, gain, twist, untwist, c_hi, c_lo, s_hi, s_lo, out,
                 ext, g_s, o_s, a_all, a_h):
    blocks, piece, rows = out.shape
    half = blocks + 1
    taps = kern.shape[1]
    tile = min(piece, 8)
    unrolled = blocks <= 16
    f32 = jnp.float32
    lane = lax.broadcasted_iota(jnp.int32, (blocks, piece, rows), 2)
    ext[0] = jnp.zeros((piece, rows), f32)

    def conv(stream, weights):
        x = sig[:, stream].astype(f32)
        total = kern[weights, 0] * x
        for lag in range(1, taps):
            rolled = pltpu.roll(x, lag, 2)
            ext[pl.ds(1, blocks)] = rolled
            earlier = jnp.where(lane < lag, ext[pl.ds(0, blocks)], rolled)
            total = total + kern[weights, lag] * earlier
        return total

    g_s[...] = conv(0, 0) * conv(1, 2)
    o_s[...] = conv(2, 1)

    def load_block(which, d, at):
        if which == 0:
            return g_s[d, at, :]
        return sig[d, 3, at, :].astype(f32)

    for tile_index in range(piece // tile):
        at = pl.ds(tile_index * tile, tile)
        for which in range(2):
            base = which * half * piece
            if unrolled:
                xs = [(load_block(which, d, at), None) for d in range(blocks)]
                spectrum = fft(xs + [(None, None)] * blocks, -1.0)
                for k in range(half):
                    for part in range(2):
                        value = spectrum[k][part]
                        if value is None:
                            value = jnp.zeros((tile, rows), f32)
                        a_all[pl.ds(base + k * piece + tile_index * tile, tile), pl.ds(part * rows, rows)] = value
            else:
                for k in range(half):
                    for part in range(2):
                        a_all[pl.ds(base + k * piece + tile_index * tile, tile), pl.ds(part * rows, rows)] = (
                            jnp.zeros((tile, rows), f32))

                def step(d, carry):
                    xd = load_block(which, d, at)
                    for k in range(half):
                        for part in range(2):
                            where = (pl.ds(base + k * piece + tile_index * tile, tile), pl.ds(part * rows, rows))
                            a_all[where] = a_all[where] + first[part * half + k, d] * xd
                    return carry

                lax.fori_loop(0, blocks, step, 0)

    for which in range(2):
        for k in range(half):
            at_rows = pl.ds(which * half * piece + k * piece, piece)
            re = a_all[at_rows, pl.ds(0, rows)]
            im = a_all[at_rows, pl.ds(rows, rows)]
            t_re = twist[0, k]
            t_im = twist[1, k]
            a_all[at_rows, pl.ds(0, rows)] = re * t_re - im * t_im
            a_all[at_rows, pl.ds(rows, rows)] = re * t_im + im * t_re
    re = halves(a_all[:, pl.ds(0, rows)])
    im = halves(a_all[:, pl.ds(rows, rows)])
    x_re = times(re, c_hi, c_lo) + times(im, s_hi, s_lo)
    x_im = times(im, c_hi, c_lo) - times(re, s_hi, s_lo)
    count = half * piece
    gr, gi = x_re[:count], x_im[:count]
    hr, hi = x_re[count:], x_im[count:]
    q_re = halves(gr * hr - gi * hi)
    q_im = halves(gr * hi + gi * hr)
    y_re = times(q_re, c_hi, c_lo) - times(q_im, s_hi, s_lo)
    y_im = times(q_re, s_hi, s_lo) + times(q_im, c_hi, c_lo)
    for k in range(half):
        at_rows = pl.ds(k * piece, piece)
        u_re = untwist[0, k]
        u_im = untwist[1, k]
        yr = y_re[k * piece:(k + 1) * piece]
        yi = y_im[k * piece:(k + 1) * piece]
        a_h[at_rows, pl.ds(0, rows)] = yr * u_re - yi * u_im
        a_h[at_rows, pl.ds(rows, rows)] = yr * u_im + yi * u_re

    for tile_index in range(piece // tile):
        at = pl.ds(tile_index * tile, tile)
        scale = gain[at]

        def finish(d, us):
            acc = None
            for k in range(half):
                for part in range(2):
                    term = last[d, part * half + k] * us(k, part)
                    acc = term if acc is None else acc + term
            gated = g_s[d, at, :]
            out[d, at, :] = (o_s[d, at, :] * (acc + scale * gated)).astype(out.dtype)

        if unrolled:
            held = [
                tuple(a_h[pl.ds(k * piece + tile_index * tile, tile), pl.ds(part * rows, rows)]
                      for part in range(2))
                for k in range(half)
            ]
            full = held + [(re, -im) for re, im in reversed(held[1:blocks])]
            signal = fft(full, 1.0)
            for d in range(blocks):
                gated = g_s[d, at, :]
                out[d, at, :] = (o_s[d, at, :] * (signal[d][0] + scale * gated)).astype(out.dtype)
        else:
            def step(d, carry):
                finish(d, lambda k, part: a_h[
                    pl.ds(k * piece + tile_index * tile, tile), pl.ds(part * rows, rows)])
                return carry

            lax.fori_loop(0, blocks, step, 0)


def to_blocks_kernel(*refs):
    *streams, out, held = refs
    blocks, _, piece, rows = out.shape
    for index, stream in enumerate(streams):
        held[...] = jnp.transpose(stream[...].astype(jnp.float32))
        for j in range(blocks):
            out[j, index] = held[pl.ds(j * piece, piece), :].astype(out.dtype)


def from_blocks_kernel(pieces, out, held):
    blocks, piece, rows = pieces.shape
    for j in range(blocks):
        held[pl.ds(j * piece, piece), :] = pieces[j].astype(jnp.float32)
    out[...] = jnp.transpose(held[...]).astype(out.dtype)


def body(gate_stream, outer_stream, value_stream, short_weight, long_filter, skip_gain):
    rows, chans = gate_stream.shape
    blocks = lax.axis_size("ctx")
    piece = chans // blocks
    half = blocks + 1
    me = lax.axis_index("ctx")
    first, last, twist, untwist, c_hi, c_lo, s_hi, s_lo = kernel_tables(blocks, rows)

    vmem = pl.BlockSpec(memory_space=pltpu.VMEM)
    stacked = pl.pallas_call(
        to_blocks_kernel,
        out_shape=jax.ShapeDtypeStruct((blocks, 4, piece, rows), jnp.bfloat16),
        in_specs=[vmem] * 4,
        out_specs=vmem,
        scratch_shapes=[pltpu.VMEM((chans, rows), jnp.float32)],
    )(gate_stream, value_stream, outer_stream, long_filter)
    gathered = lax.all_to_all(stacked, "ctx", 0, 0)

    kern = lax.dynamic_slice_in_dim(short_weight, me * piece, piece, axis=2).astype(jnp.float32)
    kern = kern[..., None]
    gain = lax.dynamic_slice_in_dim(skip_gain, me * piece, piece)[:, None]

    smem = pl.BlockSpec(memory_space=pltpu.SMEM)
    f32 = jnp.float32
    out = pl.pallas_call(
        local_kernel,
        out_shape=jax.ShapeDtypeStruct((blocks, piece, rows), jnp.bfloat16),
        in_specs=[smem, smem] + [vmem] * 9,
        out_specs=vmem,
        scratch_shapes=[
            pltpu.VMEM((blocks + 1, piece, rows), f32),
            pltpu.VMEM((blocks, piece, rows), f32),
            pltpu.VMEM((blocks, piece, rows), f32),
            pltpu.VMEM((2 * half * piece, 2 * rows), f32),
            pltpu.VMEM((half * piece, 2 * rows), f32),
        ],
    )(first, last, gathered, kern, gain, twist, untwist, c_hi, c_lo, s_hi, s_lo)

    returned = lax.all_to_all(out, "ctx", 0, 0)
    return pl.pallas_call(
        from_blocks_kernel,
        out_shape=jax.ShapeDtypeStruct((rows, chans), jnp.bfloat16),
        in_specs=[vmem],
        out_specs=vmem,
        scratch_shapes=[pltpu.VMEM((chans, rows), jnp.float32)],
    )(returned)


def solution(mesh):
    placed = (
        P(("groups", "ctx"), "ch"),
        P(("groups", "ctx"), "ch"),
        P(("groups", "ctx"), "ch"),
        P(None, None, "ch"),
        P("ctx", "ch"),
        P("ch"),
    )
    return jax.shard_map(
        body, mesh=mesh, in_specs=placed, out_specs=P(("groups", "ctx"), "ch"), check_vma=False
    )
```

```python
import math

import ml_dtypes
import numpy as np

import jax
import jax.numpy as jnp
from jax import lax
from jax.experimental import pallas as pl
from jax.experimental.pallas import tpu as pltpu
from jax.sharding import PartitionSpec as P

full_precision = lax.Precision.HIGHEST


def split_table(table):
    high = table.astype(ml_dtypes.bfloat16)
    low = (table - high.astype(np.float64)).astype(ml_dtypes.bfloat16)
    return jnp.asarray(high), jnp.asarray(low)


def kernel_tables(blocks, rows):
    total = 2 * blocks * rows
    half = blocks + 1
    k2 = np.arange(half)
    d = np.arange(blocks)
    r = np.arange(rows)
    clean = lambda a: np.where(np.abs(a) < 1e-12, 0.0, a)
    block_angle = 2.0 * np.pi * np.outer(k2, d) / (2 * blocks)
    first = clean(np.concatenate([np.cos(block_angle), -np.sin(block_angle)], axis=0))
    twist_angle = -2.0 * np.pi * np.outer(k2, r) / total
    twist = np.stack([np.cos(twist_angle), np.sin(twist_angle)])[:, :, None, :]
    untwist = np.stack([np.cos(twist_angle), -np.sin(twist_angle)])[:, :, None, :] / total
    row_angle = 2.0 * np.pi * np.outer(r, r) / rows
    weight = np.full(half, 2.0)
    weight[0] = 1.0
    weight[-1] = 1.0
    last_angle = 2.0 * np.pi * np.outer(d, k2) / (2 * blocks)
    last = clean(np.concatenate([weight * np.cos(last_angle), -weight * np.sin(last_angle)], axis=1))
    as_f32 = lambda a: jnp.asarray(a.astype(np.float32))
    return ((as_f32(first), as_f32(last), as_f32(twist), as_f32(untwist))
            + split_table(np.cos(row_angle)) + split_table(np.sin(row_angle)))


def scaled(terms):
    total = None
    for array, constant in terms:
        if array is None or constant == 0.0:
            continue
        if constant == 1.0:
            term = array
        elif constant == -1.0:
            term = -array
        else:
            term = constant * array
        total = term if total is None else total + term
    return total


def unit(angle):
    c, s = math.cos(angle), math.sin(angle)
    snap = lambda v: 0.0 if abs(v) < 1e-12 else (1.0 if abs(v - 1) < 1e-12 else (-1.0 if abs(v + 1) < 1e-12 else v))
    return snap(c), snap(s)


def fft(values, sign):
    count = len(values)
    if count == 1:
        return values
    even = fft(values[0::2], sign)
    odd = fft(values[1::2], sign)
    out = [None] * count
    for k in range(count // 2):
        c, s = unit(sign * 2.0 * math.pi * k / count)
        o_re, o_im = odd[k]
        t_re = scaled([(o_re, c), (o_im, -s)])
        t_im = scaled([(o_re, s), (o_im, c)])
        e_re, e_im = even[k]
        out[k] = (scaled([(e_re, 1.0), (t_re, 1.0)]), scaled([(e_im, 1.0), (t_im, 1.0)]))
        out[k + count // 2] = (scaled([(e_re, 1.0), (t_re, -1.0)]), scaled([(e_im, 1.0), (t_im, -1.0)]))
    return out


def halves(a):
    high = a.astype(jnp.bfloat16)
    return high, (a - high.astype(jnp.float32)).astype(jnp.bfloat16)


def times(parts, high_ref, low_ref):
    high, low = parts
    table = high_ref[...]
    out = jnp.dot(high, table, preferred_element_type=jnp.float32)
    out = out + jnp.dot(low, table, preferred_element_type=jnp.float32)
    return out + jnp.dot(high, low_ref[...], preferred_element_type=jnp.float32)


def local_kernel(first, last, sig_any, kern, gain, *refs):
    sources = refs[:6]
    out = refs[6]
    sig, held_tables, sems, ext, g_s, o_s, a_all, a_h = refs[7], refs[8:14], refs[14], *refs[15:]
    arrival = pltpu.make_async_copy(sig_any, sig, sems.at[6])
    arrival.start()
    loads = [pltpu.make_async_copy(src, dst, sems.at[i]) for i, (src, dst) in enumerate(zip(sources, held_tables))]
    for load in loads:
        load.start()
    twist, untwist, c_hi, c_lo, s_hi, s_lo = held_tables
    arrival.wait()
    blocks, piece, rows = out.shape
    half = blocks + 1
    taps = kern.shape[1]
    tile = min(piece, 8)
    unrolled = blocks <= 16
    f32 = jnp.float32
    lane = lax.broadcasted_iota(jnp.int32, (blocks, piece, rows), 2)
    ext[0] = jnp.zeros((piece, rows), f32)

    def conv(stream, weights):
        x = sig[:, stream].astype(f32)
        total = kern[weights, 0] * x
        for lag in range(1, taps):
            rolled = pltpu.roll(x, lag, 2)
            ext[pl.ds(1, blocks)] = rolled
            earlier = jnp.where(lane < lag, ext[pl.ds(0, blocks)], rolled)
            total = total + kern[weights, lag] * earlier
        return total

    g_s[...] = conv(0, 0) * conv(1, 2)
    o_s[...] = conv(2, 1)

    def load_block(which, d, at):
        if which == 0:
            return g_s[d, at, :]
        return sig[d, 3, at, :].astype(f32)

    for tile_index in range(piece // tile):
        at = pl.ds(tile_index * tile, tile)
        for which in range(2):
            base = which * half * piece
            if unrolled:
                xs = [(load_block(which, d, at), None) for d in range(blocks)]
                spectrum = fft(xs + [(None, None)] * blocks, -1.0)
                for k in range(half):
                    for part in range(2):
                        value = spectrum[k][part]
                        if value is None:
                            value = jnp.zeros((tile, rows), f32)
                        a_all[pl.ds(base + k * piece + tile_index * tile, tile), pl.ds(part * rows, rows)] = value
            else:
                for k in range(half):
                    for part in range(2):
                        a_all[pl.ds(base + k * piece + tile_index * tile, tile), pl.ds(part * rows, rows)] = (
                            jnp.zeros((tile, rows), f32))

                def step(d, carry):
                    xd = load_block(which, d, at)
                    for k in range(half):
                        for part in range(2):
                            where = (pl.ds(base + k * piece + tile_index * tile, tile), pl.ds(part * rows, rows))
                            a_all[where] = a_all[where] + first[part * half + k, d] * xd
                    return carry

                lax.fori_loop(0, blocks, step, 0)

    for load in loads:
        load.wait()
    for which in range(2):
        for k in range(half):
            at_rows = pl.ds(which * half * piece + k * piece, piece)
            re = a_all[at_rows, pl.ds(0, rows)]
            im = a_all[at_rows, pl.ds(rows, rows)]
            t_re = twist[0, k]
            t_im = twist[1, k]
            a_all[at_rows, pl.ds(0, rows)] = re * t_re - im * t_im
            a_all[at_rows, pl.ds(rows, rows)] = re * t_im + im * t_re
    re = halves(a_all[:, pl.ds(0, rows)])
    im = halves(a_all[:, pl.ds(rows, rows)])
    x_re = times(re, c_hi, c_lo) + times(im, s_hi, s_lo)
    x_im = times(im, c_hi, c_lo) - times(re, s_hi, s_lo)
    count = half * piece
    gr, gi = x_re[:count], x_im[:count]
    hr, hi = x_re[count:], x_im[count:]
    q_re = halves(gr * hr - gi * hi)
    q_im = halves(gr * hi + gi * hr)
    y_re = times(q_re, c_hi, c_lo) - times(q_im, s_hi, s_lo)
    y_im = times(q_re, s_hi, s_lo) + times(q_im, c_hi, c_lo)
    for k in range(half):
        at_rows = pl.ds(k * piece, piece)
        u_re = untwist[0, k]
        u_im = untwist[1, k]
        yr = y_re[k * piece:(k + 1) * piece]
        yi = y_im[k * piece:(k + 1) * piece]
        a_h[at_rows, pl.ds(0, rows)] = yr * u_re - yi * u_im
        a_h[at_rows, pl.ds(rows, rows)] = yr * u_im + yi * u_re

    for tile_index in range(piece // tile):
        at = pl.ds(tile_index * tile, tile)
        scale = gain[at]

        def finish(d, us):
            acc = None
            for k in range(half):
                for part in range(2):
                    term = last[d, part * half + k] * us(k, part)
                    acc = term if acc is None else acc + term
            gated = g_s[d, at, :]
            out[d, at, :] = (o_s[d, at, :] * (acc + scale * gated)).astype(out.dtype)

        if unrolled:
            held = [
                tuple(a_h[pl.ds(k * piece + tile_index * tile, tile), pl.ds(part * rows, rows)]
                      for part in range(2))
                for k in range(half)
            ]
            full = held + [(re, -im) for re, im in reversed(held[1:blocks])]
            signal = fft(full, 1.0)
            for d in range(blocks):
                gated = g_s[d, at, :]
                out[d, at, :] = (o_s[d, at, :] * (signal[d][0] + scale * gated)).astype(out.dtype)
        else:
            def step(d, carry):
                finish(d, lambda k, part: a_h[
                    pl.ds(k * piece + tile_index * tile, tile), pl.ds(part * rows, rows)])
                return carry

            lax.fori_loop(0, blocks, step, 0)


def to_blocks_kernel(*refs):
    *streams, out, held = refs
    blocks, _, piece, rows = out.shape
    for index, stream in enumerate(streams):
        held[...] = jnp.transpose(stream[...].astype(jnp.float32))
        for j in range(blocks):
            out[j, index] = held[pl.ds(j * piece, piece), :].astype(out.dtype)


def body(gate_stream, outer_stream, value_stream, short_weight, long_filter, skip_gain):
    rows, chans = gate_stream.shape
    blocks = lax.axis_size("ctx")
    piece = chans // blocks
    half = blocks + 1
    me = lax.axis_index("ctx")
    first, last, twist, untwist, c_hi, c_lo, s_hi, s_lo = kernel_tables(blocks, rows)

    vmem = pl.BlockSpec(memory_space=pltpu.VMEM)
    stacked = pl.pallas_call(
        to_blocks_kernel,
        out_shape=jax.ShapeDtypeStruct((blocks, 4, piece, rows), jnp.bfloat16),
        in_specs=[vmem] * 4,
        out_specs=vmem,
        scratch_shapes=[pltpu.VMEM((chans, rows), jnp.float32)],
    )(gate_stream, value_stream, outer_stream, long_filter)
    gathered = lax.all_to_all(stacked, "ctx", 0, 0)

    kern = lax.dynamic_slice_in_dim(short_weight, me * piece, piece, axis=2).astype(jnp.float32)
    kern = kern[..., None]
    gain = lax.dynamic_slice_in_dim(skip_gain, me * piece, piece)[:, None]

    smem = pl.BlockSpec(memory_space=pltpu.SMEM)
    anywhere = pl.BlockSpec(memory_space=pl.ANY)
    tables = (twist, untwist, c_hi, c_lo, s_hi, s_lo)
    f32 = jnp.float32
    out = pl.pallas_call(
        local_kernel,
        out_shape=jax.ShapeDtypeStruct((blocks, piece, rows), jnp.bfloat16),
        in_specs=[smem, smem, anywhere, vmem, vmem] + [anywhere] * 6,
        out_specs=vmem,
        scratch_shapes=[
            pltpu.VMEM(gathered.shape, gathered.dtype),
            *[pltpu.VMEM(t.shape, t.dtype) for t in tables],
            pltpu.SemaphoreType.DMA((7,)),
            pltpu.VMEM((blocks + 1, piece, rows), f32),
            pltpu.VMEM((blocks, piece, rows), f32),
            pltpu.VMEM((blocks, piece, rows), f32),
            pltpu.VMEM((2 * half * piece, 2 * rows), f32),
            pltpu.VMEM((half * piece, 2 * rows), f32),
        ],
    )(first, last, gathered, kern, gain, *tables)

    returned = lax.all_to_all(out, "ctx", 0, 0)
    return jnp.swapaxes(returned.reshape(chans, rows), 0, 1)


def solution(mesh):
    placed = (
        P(("groups", "ctx"), "ch"),
        P(("groups", "ctx"), "ch"),
        P(("groups", "ctx"), "ch"),
        P(None, None, "ch"),
        P("ctx", "ch"),
        P("ch"),
    )
    return jax.shard_map(
        body, mesh=mesh, in_specs=placed, out_specs=P(("groups", "ctx"), "ch"), check_vma=False
    )
```

```python
import math

import ml_dtypes
import numpy as np

import jax
import jax.numpy as jnp
from jax import lax
from jax.experimental import pallas as pl
from jax.experimental.pallas import tpu as pltpu
from jax.sharding import PartitionSpec as P

full_precision = lax.Precision.HIGHEST


def split_table(table):
    high = table.astype(ml_dtypes.bfloat16)
    low = (table - high.astype(np.float64)).astype(ml_dtypes.bfloat16)
    return jnp.asarray(high), jnp.asarray(low)


def kernel_tables(blocks, rows):
    total = 2 * blocks * rows
    half = blocks + 1
    k2 = np.arange(half)
    d = np.arange(blocks)
    r = np.arange(rows)
    clean = lambda a: np.where(np.abs(a) < 1e-12, 0.0, a)
    block_angle = 2.0 * np.pi * np.outer(k2, d) / (2 * blocks)
    first = clean(np.concatenate([np.cos(block_angle), -np.sin(block_angle)], axis=0))
    twist_angle = -2.0 * np.pi * np.outer(k2, r) / total
    twist = np.stack([np.cos(twist_angle), np.sin(twist_angle)])[:, :, None, :]
    untwist = np.stack([np.cos(twist_angle), -np.sin(twist_angle)])[:, :, None, :] / total
    row_angle = 2.0 * np.pi * np.outer(r, r) / rows
    weight = np.full(half, 2.0)
    weight[0] = 1.0
    weight[-1] = 1.0
    last_angle = 2.0 * np.pi * np.outer(d, k2) / (2 * blocks)
    last = clean(np.concatenate([weight * np.cos(last_angle), -weight * np.sin(last_angle)], axis=1))
    as_f32 = lambda a: jnp.asarray(a.astype(np.float32))
    return ((as_f32(first), as_f32(last), as_f32(twist), as_f32(untwist))
            + split_table(np.cos(row_angle)) + split_table(np.sin(row_angle)))


def scaled(terms):
    total = None
    for array, constant in terms:
        if array is None or constant == 0.0:
            continue
        if constant == 1.0:
            term = array
        elif constant == -1.0:
            term = -array
        else:
            term = constant * array
        total = term if total is None else total + term
    return total


def unit(angle):
    c, s = math.cos(angle), math.sin(angle)
    snap = lambda v: 0.0 if abs(v) < 1e-12 else (1.0 if abs(v - 1) < 1e-12 else (-1.0 if abs(v + 1) < 1e-12 else v))
    return snap(c), snap(s)


def fft(values, sign):
    count = len(values)
    if count == 1:
        return values
    even = fft(values[0::2], sign)
    odd = fft(values[1::2], sign)
    out = [None] * count
    for k in range(count // 2):
        c, s = unit(sign * 2.0 * math.pi * k / count)
        o_re, o_im = odd[k]
        t_re = scaled([(o_re, c), (o_im, -s)])
        t_im = scaled([(o_re, s), (o_im, c)])
        e_re, e_im = even[k]
        out[k] = (scaled([(e_re, 1.0), (t_re, 1.0)]), scaled([(e_im, 1.0), (t_im, 1.0)]))
        out[k + count // 2] = (scaled([(e_re, 1.0), (t_re, -1.0)]), scaled([(e_im, 1.0), (t_im, -1.0)]))
    return out


def halves(a):
    high = a.astype(jnp.bfloat16)
    return high, (a - high.astype(jnp.float32)).astype(jnp.bfloat16)


def times(parts, high_ref, low_ref):
    high, low = parts
    table = high_ref[...]
    out = jnp.dot(high, table, preferred_element_type=jnp.float32)
    out = out + jnp.dot(low, table, preferred_element_type=jnp.float32)
    return out + jnp.dot(high, low_ref[...], preferred_element_type=jnp.float32)


def local_kernel(first, last, sig, kern, gain, twist, untwist, c_hi, c_lo, s_hi, s_lo, out,
                 ext, g_s, o_s, a_all, a_h):
    blocks, piece, rows = out.shape
    half = blocks + 1
    taps = kern.shape[1]
    tile = min(piece, 8)
    unrolled = blocks <= 16
    f32 = jnp.float32
    lane = lax.broadcasted_iota(jnp.int32, (blocks, piece, rows), 2)
    ext[0] = jnp.zeros((piece, rows), f32)

    def conv(stream, weights):
        x = sig[:, stream].astype(f32)
        total = kern[weights, 0] * x
        for lag in range(1, taps):
            rolled = pltpu.roll(x, lag, 2)
            ext[pl.ds(1, blocks)] = rolled
            earlier = jnp.where(lane < lag, ext[pl.ds(0, blocks)], rolled)
            total = total + kern[weights, lag] * earlier
        return total

    g_s[...] = conv(0, 0) * conv(1, 2)
    o_s[...] = conv(2, 1)

    def load_block(which, d, at):
        if which == 0:
            return g_s[d, at, :]
        return sig[d, 3, at, :].astype(f32)

    for tile_index in range(piece // tile):
        at = pl.ds(tile_index * tile, tile)
        for which in range(2):
            base = which * half * piece
            if unrolled:
                xs = [(load_block(which, d, at), None) for d in range(blocks)]
                spectrum = fft(xs + [(None, None)] * blocks, -1.0)
                for k in range(half):
                    for part in range(2):
                        value = spectrum[k][part]
                        if value is None:
                            value = jnp.zeros((tile, rows), f32)
                        a_all[pl.ds(base + k * piece + tile_index * tile, tile), pl.ds(part * rows, rows)] = value
            else:
                for k in range(half):
                    for part in range(2):
                        a_all[pl.ds(base + k * piece + tile_index * tile, tile), pl.ds(part * rows, rows)] = (
                            jnp.zeros((tile, rows), f32))

                def step(d, carry):
                    xd = load_block(which, d, at)
                    for k in range(half):
                        for part in range(2):
                            where = (pl.ds(base + k * piece + tile_index * tile, tile), pl.ds(part * rows, rows))
                            a_all[where] = a_all[where] + first[part * half + k, d] * xd
                    return carry

                lax.fori_loop(0, blocks, step, 0)

    for which in range(2):
        for k in range(half):
            at_rows = pl.ds(which * half * piece + k * piece, piece)
            re = a_all[at_rows, pl.ds(0, rows)]
            im = a_all[at_rows, pl.ds(rows, rows)]
            t_re = twist[0, k]
            t_im = twist[1, k]
            a_all[at_rows, pl.ds(0, rows)] = re * t_re - im * t_im
            a_all[at_rows, pl.ds(rows, rows)] = re * t_im + im * t_re
    re = halves(a_all[:, pl.ds(0, rows)])
    im = halves(a_all[:, pl.ds(rows, rows)])
    x_re = times(re, c_hi, c_lo) + times(im, s_hi, s_lo)
    x_im = times(im, c_hi, c_lo) - times(re, s_hi, s_lo)
    count = half * piece
    gr, gi = x_re[:count], x_im[:count]
    hr, hi = x_re[count:], x_im[count:]
    q_re = halves(gr * hr - gi * hi)
    q_im = halves(gr * hi + gi * hr)
    y_re = times(q_re, c_hi, c_lo) - times(q_im, s_hi, s_lo)
    y_im = times(q_re, s_hi, s_lo) + times(q_im, c_hi, c_lo)
    for k in range(half):
        at_rows = pl.ds(k * piece, piece)
        u_re = untwist[0, k]
        u_im = untwist[1, k]
        yr = y_re[k * piece:(k + 1) * piece]
        yi = y_im[k * piece:(k + 1) * piece]
        a_h[at_rows, pl.ds(0, rows)] = yr * u_re - yi * u_im
        a_h[at_rows, pl.ds(rows, rows)] = yr * u_im + yi * u_re

    for tile_index in range(piece // tile):
        at = pl.ds(tile_index * tile, tile)
        scale = gain[at]

        def finish(d, us):
            acc = None
            for k in range(half):
                for part in range(2):
                    term = last[d, part * half + k] * us(k, part)
                    acc = term if acc is None else acc + term
            gated = g_s[d, at, :]
            out[d, at, :] = (o_s[d, at, :] * (acc + scale * gated)).astype(out.dtype)

        if unrolled:
            held = [
                tuple(a_h[pl.ds(k * piece + tile_index * tile, tile), pl.ds(part * rows, rows)]
                      for part in range(2))
                for k in range(half)
            ]
            full = held + [(re, -im) for re, im in reversed(held[1:blocks])]
            signal = fft(full, 1.0)
            for d in range(blocks):
                gated = g_s[d, at, :]
                out[d, at, :] = (o_s[d, at, :] * (signal[d][0] + scale * gated)).astype(out.dtype)
        else:
            def step(d, carry):
                finish(d, lambda k, part: a_h[
                    pl.ds(k * piece + tile_index * tile, tile), pl.ds(part * rows, rows)])
                return carry

            lax.fori_loop(0, blocks, step, 0)


def to_blocks_kernel(*refs):
    *streams, out, held = refs
    blocks, _, piece, rows = out.shape
    chans = held.shape[0]
    eye = (lax.broadcasted_iota(jnp.int32, (chans, chans), 0)
           == lax.broadcasted_iota(jnp.int32, (chans, chans), 1)).astype(jnp.bfloat16)
    for index, stream in enumerate(streams):
        held[...] = lax.dot_general(eye, stream[...], (((1,), (1,)), ((), ())),
                                    preferred_element_type=jnp.float32)
        for j in range(blocks):
            out[j, index] = held[pl.ds(j * piece, piece), :].astype(out.dtype)


def body(gate_stream, outer_stream, value_stream, short_weight, long_filter, skip_gain):
    rows, chans = gate_stream.shape
    blocks = lax.axis_size("ctx")
    piece = chans // blocks
    half = blocks + 1
    me = lax.axis_index("ctx")
    first, last, twist, untwist, c_hi, c_lo, s_hi, s_lo = kernel_tables(blocks, rows)

    vmem = pl.BlockSpec(memory_space=pltpu.VMEM)
    stacked = pl.pallas_call(
        to_blocks_kernel,
        out_shape=jax.ShapeDtypeStruct((blocks, 4, piece, rows), jnp.bfloat16),
        in_specs=[vmem] * 4,
        out_specs=vmem,
        scratch_shapes=[pltpu.VMEM((chans, rows), jnp.float32)],
    )(gate_stream, value_stream, outer_stream, long_filter)
    gathered = lax.all_to_all(stacked, "ctx", 0, 0)

    kern = lax.dynamic_slice_in_dim(short_weight, me * piece, piece, axis=2).astype(jnp.float32)
    kern = kern[..., None]
    gain = lax.dynamic_slice_in_dim(skip_gain, me * piece, piece)[:, None]

    smem = pl.BlockSpec(memory_space=pltpu.SMEM)
    f32 = jnp.float32
    out = pl.pallas_call(
        local_kernel,
        out_shape=jax.ShapeDtypeStruct((blocks, piece, rows), jnp.bfloat16),
        in_specs=[smem, smem] + [vmem] * 9,
        out_specs=vmem,
        scratch_shapes=[
            pltpu.VMEM((blocks + 1, piece, rows), f32),
            pltpu.VMEM((blocks, piece, rows), f32),
            pltpu.VMEM((blocks, piece, rows), f32),
            pltpu.VMEM((2 * half * piece, 2 * rows), f32),
            pltpu.VMEM((half * piece, 2 * rows), f32),
        ],
    )(first, last, gathered, kern, gain, twist, untwist, c_hi, c_lo, s_hi, s_lo)

    returned = lax.all_to_all(out, "ctx", 0, 0)
    return jnp.swapaxes(returned.reshape(chans, rows), 0, 1)


def solution(mesh):
    placed = (
        P(("groups", "ctx"), "ch"),
        P(("groups", "ctx"), "ch"),
        P(("groups", "ctx"), "ch"),
        P(None, None, "ch"),
        P("ctx", "ch"),
        P("ch"),
    )
    return jax.shard_map(
        body, mesh=mesh, in_specs=placed, out_specs=P(("groups", "ctx"), "ch"), check_vma=False
    )
```

```python
import math

import ml_dtypes
import numpy as np

import jax
import jax.numpy as jnp
from jax import lax
from jax.experimental import pallas as pl
from jax.experimental.pallas import tpu as pltpu
from jax.sharding import PartitionSpec as P

full_precision = lax.Precision.HIGHEST


def split_table(table):
    high = table.astype(ml_dtypes.bfloat16)
    low = (table - high.astype(np.float64)).astype(ml_dtypes.bfloat16)
    return jnp.asarray(high), jnp.asarray(low)


def kernel_tables(blocks, rows):
    total = 2 * blocks * rows
    half = blocks + 1
    k2 = np.arange(half)
    d = np.arange(blocks)
    r = np.arange(rows)
    clean = lambda a: np.where(np.abs(a) < 1e-12, 0.0, a)
    block_angle = 2.0 * np.pi * np.outer(k2, d) / (2 * blocks)
    first = clean(np.concatenate([np.cos(block_angle), -np.sin(block_angle)], axis=0))
    twist_angle = -2.0 * np.pi * np.outer(k2, r) / total
    twist = np.stack([np.cos(twist_angle), np.sin(twist_angle)])[:, :, None, :]
    untwist = np.stack([np.cos(twist_angle), -np.sin(twist_angle)])[:, :, None, :] / total
    row_angle = 2.0 * np.pi * np.outer(r, r) / rows
    weight = np.full(half, 2.0)
    weight[0] = 1.0
    weight[-1] = 1.0
    last_angle = 2.0 * np.pi * np.outer(d, k2) / (2 * blocks)
    last = clean(np.concatenate([weight * np.cos(last_angle), -weight * np.sin(last_angle)], axis=1))
    as_f32 = lambda a: jnp.asarray(a.astype(np.float32))
    return ((as_f32(first), as_f32(last), as_f32(twist), as_f32(untwist))
            + split_table(np.cos(row_angle)) + split_table(np.sin(row_angle)))


def scaled(terms):
    total = None
    for array, constant in terms:
        if array is None or constant == 0.0:
            continue
        if constant == 1.0:
            term = array
        elif constant == -1.0:
            term = -array
        else:
            term = constant * array
        total = term if total is None else total + term
    return total


def unit(angle):
    c, s = math.cos(angle), math.sin(angle)
    snap = lambda v: 0.0 if abs(v) < 1e-12 else (1.0 if abs(v - 1) < 1e-12 else (-1.0 if abs(v + 1) < 1e-12 else v))
    return snap(c), snap(s)


def fft(values, sign):
    count = len(values)
    if count == 1:
        return values
    even = fft(values[0::2], sign)
    odd = fft(values[1::2], sign)
    out = [None] * count
    for k in range(count // 2):
        c, s = unit(sign * 2.0 * math.pi * k / count)
        o_re, o_im = odd[k]
        t_re = scaled([(o_re, c), (o_im, -s)])
        t_im = scaled([(o_re, s), (o_im, c)])
        e_re, e_im = even[k]
        out[k] = (scaled([(e_re, 1.0), (t_re, 1.0)]), scaled([(e_im, 1.0), (t_im, 1.0)]))
        out[k + count // 2] = (scaled([(e_re, 1.0), (t_re, -1.0)]), scaled([(e_im, 1.0), (t_im, -1.0)]))
    return out


def halves(a):
    high = a.astype(jnp.bfloat16)
    return high, (a - high.astype(jnp.float32)).astype(jnp.bfloat16)


def times(parts, high_ref, low_ref):
    high, low = parts
    table = high_ref[...]
    out = jnp.dot(high, table, preferred_element_type=jnp.float32)
    out = out + jnp.dot(low, table, preferred_element_type=jnp.float32)
    return out + jnp.dot(high, low_ref[...], preferred_element_type=jnp.float32)


def local_kernel(first, last, sig, kern, gain, twist, untwist, c_hi, c_lo, s_hi, s_lo, out,
                 ext, g_s, o_s, a_all, a_h):
    blocks, piece, rows = out.shape
    half = blocks + 1
    taps = kern.shape[1]
    tile = min(piece, 8)
    unrolled = blocks <= 16
    f32 = jnp.float32
    lane = lax.broadcasted_iota(jnp.int32, (blocks, piece, rows), 2)

    def conv(stream, weights):
        x = sig[:, stream].astype(f32)
        total = kern[weights, 0] * x
        for lag in range(1, taps):
            rolled = pltpu.roll(x, lag, 2)
            before = jnp.concatenate([jnp.zeros_like(rolled[:1]), rolled[:-1]], axis=0)
            earlier = jnp.where(lane < lag, before, rolled)
            total = total + kern[weights, lag] * earlier
        return total

    g_s[...] = conv(0, 0) * conv(1, 2)
    o_s[...] = conv(2, 1)

    def load_block(which, d, at):
        if which == 0:
            return g_s[d, at, :]
        return sig[d, 3, at, :].astype(f32)

    for tile_index in range(piece // tile):
        at = pl.ds(tile_index * tile, tile)
        for which in range(2):
            base = which * half * piece
            if unrolled:
                xs = [(load_block(which, d, at), None) for d in range(blocks)]
                spectrum = fft(xs + [(None, None)] * blocks, -1.0)
                for k in range(half):
                    c, s = twist[0, k], twist[1, k]
                    re, im = spectrum[k]
                    if im is None:
                        turned = (re * c, re * s)
                    elif re is None:
                        turned = (-(im * s), im * c)
                    else:
                        turned = (re * c - im * s, re * s + im * c)
                    for part in range(2):
                        a_all[pl.ds(base + k * piece + tile_index * tile, tile), pl.ds(part * rows, rows)] = (
                            turned[part])
            else:
                for k in range(half):
                    for part in range(2):
                        a_all[pl.ds(base + k * piece + tile_index * tile, tile), pl.ds(part * rows, rows)] = (
                            jnp.zeros((tile, rows), f32))

                def step(d, carry):
                    xd = load_block(which, d, at)
                    for k in range(half):
                        for part in range(2):
                            where = (pl.ds(base + k * piece + tile_index * tile, tile), pl.ds(part * rows, rows))
                            a_all[where] = a_all[where] + first[part * half + k, d] * xd
                    return carry

                lax.fori_loop(0, blocks, step, 0)

    for which in range(0 if unrolled else 2):
        for k in range(half):
            at_rows = pl.ds(which * half * piece + k * piece, piece)
            re = a_all[at_rows, pl.ds(0, rows)]
            im = a_all[at_rows, pl.ds(rows, rows)]
            t_re = twist[0, k]
            t_im = twist[1, k]
            a_all[at_rows, pl.ds(0, rows)] = re * t_re - im * t_im
            a_all[at_rows, pl.ds(rows, rows)] = re * t_im + im * t_re
    re = halves(a_all[:, pl.ds(0, rows)])
    im = halves(a_all[:, pl.ds(rows, rows)])
    x_re = times(re, c_hi, c_lo) + times(im, s_hi, s_lo)
    x_im = times(im, c_hi, c_lo) - times(re, s_hi, s_lo)
    count = half * piece
    gr, gi = x_re[:count], x_im[:count]
    hr, hi = x_re[count:], x_im[count:]
    q_re = halves(gr * hr - gi * hi)
    q_im = halves(gr * hi + gi * hr)
    y_re = times(q_re, c_hi, c_lo) - times(q_im, s_hi, s_lo)
    y_im = times(q_re, s_hi, s_lo) + times(q_im, c_hi, c_lo)
    def untwisted(k, at_tile):
        lo = k * piece + at_tile * tile
        yr = y_re[lo:lo + tile]
        yi = y_im[lo:lo + tile]
        u_re = untwist[0, k]
        u_im = untwist[1, k]
        return yr * u_re - yi * u_im, yr * u_im + yi * u_re

    if not unrolled:
        for k in range(half):
            at_rows = pl.ds(k * piece, piece)
            yr = y_re[k * piece:(k + 1) * piece]
            yi = y_im[k * piece:(k + 1) * piece]
            a_h[at_rows, pl.ds(0, rows)] = yr * untwist[0, k] - yi * untwist[1, k]
            a_h[at_rows, pl.ds(rows, rows)] = yr * untwist[1, k] + yi * untwist[0, k]

    for tile_index in range(piece // tile):
        at = pl.ds(tile_index * tile, tile)
        scale = gain[at]

        def finish(d, us):
            acc = None
            for k in range(half):
                for part in range(2):
                    term = last[d, part * half + k] * us(k, part)
                    acc = term if acc is None else acc + term
            gated = g_s[d, at, :]
            out[d, at, :] = (o_s[d, at, :] * (acc + scale * gated)).astype(out.dtype)

        if unrolled:
            held = [untwisted(k, tile_index) for k in range(half)]
            full = held + [(re, -im) for re, im in reversed(held[1:blocks])]
            signal = fft(full, 1.0)
            for d in range(blocks):
                gated = g_s[d, at, :]
                out[d, at, :] = (o_s[d, at, :] * (signal[d][0] + scale * gated)).astype(out.dtype)
        else:
            def step(d, carry):
                finish(d, lambda k, part: a_h[
                    pl.ds(k * piece + tile_index * tile, tile), pl.ds(part * rows, rows)])
                return carry

            lax.fori_loop(0, blocks, step, 0)


def to_blocks_kernel(*refs):
    *streams, out, held = refs
    blocks, _, piece, rows = out.shape
    chans = held.shape[0]
    eye = (lax.broadcasted_iota(jnp.int32, (chans, chans), 0)
           == lax.broadcasted_iota(jnp.int32, (chans, chans), 1)).astype(jnp.bfloat16)
    for index, stream in enumerate(streams):
        held[...] = lax.dot_general(eye, stream[...], (((1,), (1,)), ((), ())),
                                    preferred_element_type=jnp.float32)
        for j in range(blocks):
            out[j, index] = held[pl.ds(j * piece, piece), :].astype(out.dtype)


def body(gate_stream, outer_stream, value_stream, short_weight, long_filter, skip_gain):
    rows, chans = gate_stream.shape
    blocks = lax.axis_size("ctx")
    piece = chans // blocks
    half = blocks + 1
    me = lax.axis_index("ctx")
    first, last, twist, untwist, c_hi, c_lo, s_hi, s_lo = kernel_tables(blocks, rows)

    vmem = pl.BlockSpec(memory_space=pltpu.VMEM)
    stacked = pl.pallas_call(
        to_blocks_kernel,
        out_shape=jax.ShapeDtypeStruct((blocks, 4, piece, rows), jnp.bfloat16),
        in_specs=[vmem] * 4,
        out_specs=vmem,
        scratch_shapes=[pltpu.VMEM((chans, rows), jnp.float32)],
    )(gate_stream, value_stream, outer_stream, long_filter)
    gathered = lax.all_to_all(stacked, "ctx", 0, 0)

    kern = lax.dynamic_slice_in_dim(short_weight, me * piece, piece, axis=2).astype(jnp.float32)
    kern = kern[..., None]
    gain = lax.dynamic_slice_in_dim(skip_gain, me * piece, piece)[:, None]

    smem = pl.BlockSpec(memory_space=pltpu.SMEM)
    f32 = jnp.float32
    out = pl.pallas_call(
        local_kernel,
        out_shape=jax.ShapeDtypeStruct((blocks, piece, rows), jnp.bfloat16),
        in_specs=[smem, smem] + [vmem] * 9,
        out_specs=vmem,
        scratch_shapes=[
            pltpu.VMEM((blocks + 1, piece, rows), f32),
            pltpu.VMEM((blocks, piece, rows), f32),
            pltpu.VMEM((blocks, piece, rows), f32),
            pltpu.VMEM((2 * half * piece, 2 * rows), f32),
            pltpu.VMEM((half * piece, 2 * rows), f32),
        ],
    )(first, last, gathered, kern, gain, twist, untwist, c_hi, c_lo, s_hi, s_lo)

    returned = lax.all_to_all(out, "ctx", 0, 0)
    return jnp.swapaxes(returned.reshape(chans, rows), 0, 1)


def solution(mesh):
    placed = (
        P(("groups", "ctx"), "ch"),
        P(("groups", "ctx"), "ch"),
        P(("groups", "ctx"), "ch"),
        P(None, None, "ch"),
        P("ctx", "ch"),
        P("ch"),
    )
    return jax.shard_map(
        body, mesh=mesh, in_specs=placed, out_specs=P(("groups", "ctx"), "ch"), check_vma=False
    )
```

```python
import math

import ml_dtypes
import numpy as np

import jax
import jax.numpy as jnp
from jax import lax
from jax.experimental import pallas as pl
from jax.experimental.pallas import tpu as pltpu
from jax.sharding import PartitionSpec as P

full_precision = lax.Precision.HIGHEST


def split_table(table):
    high = table.astype(ml_dtypes.bfloat16)
    low = (table - high.astype(np.float64)).astype(ml_dtypes.bfloat16)
    return jnp.asarray(high), jnp.asarray(low)


def kernel_tables(blocks, rows):
    total = 2 * blocks * rows
    half = blocks + 1
    k2 = np.arange(half)
    d = np.arange(blocks)
    r = np.arange(rows)
    clean = lambda a: np.where(np.abs(a) < 1e-12, 0.0, a)
    block_angle = 2.0 * np.pi * np.outer(k2, d) / (2 * blocks)
    first = clean(np.concatenate([np.cos(block_angle), -np.sin(block_angle)], axis=0))
    twist_angle = -2.0 * np.pi * np.outer(k2, r) / total
    twist = np.stack([np.cos(twist_angle), np.sin(twist_angle)])[:, :, None, :]
    untwist = np.stack([np.cos(twist_angle), -np.sin(twist_angle)])[:, :, None, :] / total
    row_angle = 2.0 * np.pi * np.outer(r, r) / rows
    weight = np.full(half, 2.0)
    weight[0] = 1.0
    weight[-1] = 1.0
    last_angle = 2.0 * np.pi * np.outer(d, k2) / (2 * blocks)
    last = clean(np.concatenate([weight * np.cos(last_angle), -weight * np.sin(last_angle)], axis=1))
    as_f32 = lambda a: jnp.asarray(a.astype(np.float32))
    return ((as_f32(first), as_f32(last), as_f32(twist), as_f32(untwist))
            + split_table(np.cos(row_angle)) + split_table(np.sin(row_angle)))


def scaled(terms):
    total = None
    for array, constant in terms:
        if array is None or constant == 0.0:
            continue
        if constant == 1.0:
            term = array
        elif constant == -1.0:
            term = -array
        else:
            term = constant * array
        total = term if total is None else total + term
    return total


def unit(angle):
    c, s = math.cos(angle), math.sin(angle)
    snap = lambda v: 0.0 if abs(v) < 1e-12 else (1.0 if abs(v - 1) < 1e-12 else (-1.0 if abs(v + 1) < 1e-12 else v))
    return snap(c), snap(s)


def fft(values, sign):
    count = len(values)
    if count == 1:
        return values
    even = fft(values[0::2], sign)
    odd = fft(values[1::2], sign)
    out = [None] * count
    for k in range(count // 2):
        c, s = unit(sign * 2.0 * math.pi * k / count)
        o_re, o_im = odd[k]
        t_re = scaled([(o_re, c), (o_im, -s)])
        t_im = scaled([(o_re, s), (o_im, c)])
        e_re, e_im = even[k]
        out[k] = (scaled([(e_re, 1.0), (t_re, 1.0)]), scaled([(e_im, 1.0), (t_im, 1.0)]))
        out[k + count // 2] = (scaled([(e_re, 1.0), (t_re, -1.0)]), scaled([(e_im, 1.0), (t_im, -1.0)]))
    return out


def halves(a):
    high = a.astype(jnp.bfloat16)
    return high, (a - high.astype(jnp.float32)).astype(jnp.bfloat16)


def times(parts, high_ref, low_ref):
    high, low = parts
    table = high_ref[...]
    out = jnp.dot(high, table, preferred_element_type=jnp.float32)
    out = out + jnp.dot(low, table, preferred_element_type=jnp.float32)
    return out + jnp.dot(high, low_ref[...], preferred_element_type=jnp.float32)


def local_kernel(first, last, sig, kern, gain, twist, untwist, c_hi, c_lo, s_hi, s_lo, out,
                 ext, g_s, o_s, a_all, a_h):
    blocks, piece, rows = out.shape
    half = blocks + 1
    taps = kern.shape[1]
    tile = min(piece, 8)
    unrolled = blocks <= 16
    f32 = jnp.float32
    lane = lax.broadcasted_iota(jnp.int32, (blocks, piece, rows), 2)

    def conv(stream, weights):
        x = sig[:, stream].astype(f32)
        total = kern[weights, 0] * x
        for lag in range(1, taps):
            rolled = pltpu.roll(x, lag, 2)
            before = jnp.concatenate([jnp.zeros_like(rolled[:1]), rolled[:-1]], axis=0)
            earlier = jnp.where(lane < lag, before, rolled)
            total = total + kern[weights, lag] * earlier
        return total

    g_s[...] = conv(0, 0) * conv(1, 2)
    o_s[...] = conv(2, 1)

    def load_block(which, d, at):
        if which == 0:
            return g_s[d, at, :]
        return sig[d, 3, at, :].astype(f32)

    for tile_index in range(piece // tile):
        at = pl.ds(tile_index * tile, tile)
        for which in range(2):
            base = which * half * piece
            if unrolled:
                xs = [(load_block(which, d, at), None) for d in range(blocks)]
                spectrum = fft(xs + [(None, None)] * blocks, -1.0)
                for k in range(half):
                    c, s = twist[0, k], twist[1, k]
                    re, im = spectrum[k]
                    if im is None:
                        turned = (re * c, re * s)
                    elif re is None:
                        turned = (-(im * s), im * c)
                    else:
                        turned = (re * c - im * s, re * s + im * c)
                    for part in range(2):
                        a_all[pl.ds(base + k * piece + tile_index * tile, tile), pl.ds(part * rows, rows)] = (
                            turned[part])
            else:
                for k in range(half):
                    for part in range(2):
                        a_all[pl.ds(base + k * piece + tile_index * tile, tile), pl.ds(part * rows, rows)] = (
                            jnp.zeros((tile, rows), f32))

                def step(d, carry):
                    xd = load_block(which, d, at)
                    for k in range(half):
                        for part in range(2):
                            where = (pl.ds(base + k * piece + tile_index * tile, tile), pl.ds(part * rows, rows))
                            a_all[where] = a_all[where] + first[part * half + k, d] * xd
                    return carry

                lax.fori_loop(0, blocks, step, 0)

    for which in range(0 if unrolled else 2):
        for k in range(half):
            at_rows = pl.ds(which * half * piece + k * piece, piece)
            re = a_all[at_rows, pl.ds(0, rows)]
            im = a_all[at_rows, pl.ds(rows, rows)]
            t_re = twist[0, k]
            t_im = twist[1, k]
            a_all[at_rows, pl.ds(0, rows)] = re * t_re - im * t_im
            a_all[at_rows, pl.ds(rows, rows)] = re * t_im + im * t_re
    re = halves(a_all[:, pl.ds(0, rows)])
    im = halves(a_all[:, pl.ds(rows, rows)])
    x_re = times(re, c_hi, c_lo) + times(im, s_hi, s_lo)
    x_im = times(im, c_hi, c_lo) - times(re, s_hi, s_lo)
    count = half * piece
    gr, gi = x_re[:count], x_im[:count]
    hr, hi = x_re[count:], x_im[count:]
    q_re = halves(gr * hr - gi * hi)
    q_im = halves(gr * hi + gi * hr)
    y_re = times(q_re, c_hi, c_lo) - times(q_im, s_hi, s_lo)
    y_im = times(q_re, s_hi, s_lo) + times(q_im, c_hi, c_lo)
    def untwisted(k, at_tile):
        lo = k * piece + at_tile * tile
        yr = y_re[lo:lo + tile]
        yi = y_im[lo:lo + tile]
        u_re = untwist[0, k]
        u_im = untwist[1, k]
        return yr * u_re - yi * u_im, yr * u_im + yi * u_re

    if not unrolled:
        for k in range(half):
            at_rows = pl.ds(k * piece, piece)
            yr = y_re[k * piece:(k + 1) * piece]
            yi = y_im[k * piece:(k + 1) * piece]
            a_h[at_rows, pl.ds(0, rows)] = yr * untwist[0, k] - yi * untwist[1, k]
            a_h[at_rows, pl.ds(rows, rows)] = yr * untwist[1, k] + yi * untwist[0, k]

    for tile_index in range(piece // tile):
        at = pl.ds(tile_index * tile, tile)
        scale = gain[at]

        def finish(d, us):
            acc = None
            for k in range(half):
                for part in range(2):
                    term = last[d, part * half + k] * us(k, part)
                    acc = term if acc is None else acc + term
            gated = g_s[d, at, :]
            out[d, at, :] = (o_s[d, at, :] * (acc + scale * gated)).astype(out.dtype)

        if unrolled:
            held = [untwisted(k, tile_index) for k in range(half)]
            full = held + [(re, -im) for re, im in reversed(held[1:blocks])]
            signal = fft(full, 1.0)
            for d in range(blocks):
                gated = g_s[d, at, :]
                out[d, at, :] = (o_s[d, at, :] * (signal[d][0] + scale * gated)).astype(out.dtype)
        else:
            def step(d, carry):
                finish(d, lambda k, part: a_h[
                    pl.ds(k * piece + tile_index * tile, tile), pl.ds(part * rows, rows)])
                return carry

            lax.fori_loop(0, blocks, step, 0)


def to_blocks_kernel(*refs):
    *streams, out, held = refs
    blocks, _, piece, rows = out.shape
    chans = held.shape[0]
    eye = (lax.broadcasted_iota(jnp.int32, (chans, chans), 0)
           == lax.broadcasted_iota(jnp.int32, (chans, chans), 1)).astype(jnp.bfloat16)
    for index, stream in enumerate(streams):
        held[...] = lax.dot_general(eye, stream[...], (((1,), (1,)), ((), ())),
                                    preferred_element_type=jnp.float32)
        for j in range(blocks):
            out[j, index] = held[pl.ds(j * piece, piece), :].astype(out.dtype)


def body(gate_stream, outer_stream, value_stream, short_weight, long_filter, skip_gain):
    rows, chans = gate_stream.shape
    blocks = lax.axis_size("ctx")
    piece = chans // blocks
    half = blocks + 1
    me = lax.axis_index("ctx")
    first, last, twist, untwist, c_hi, c_lo, s_hi, s_lo = kernel_tables(blocks, rows)

    vmem = pl.BlockSpec(memory_space=pltpu.VMEM)
    stacked = pl.pallas_call(
        to_blocks_kernel,
        out_shape=jax.ShapeDtypeStruct((blocks, 4, piece, rows), jnp.bfloat16),
        in_specs=[vmem] * 4,
        out_specs=vmem,
        scratch_shapes=[pltpu.VMEM((chans, rows), jnp.float32)],
    )(gate_stream, value_stream, outer_stream, long_filter)
    gathered = lax.all_to_all(stacked, "ctx", 0, 0)

    kern = lax.dynamic_slice_in_dim(short_weight, me * piece, piece, axis=2).astype(jnp.float32)
    kern = kern[..., None]
    gain = lax.dynamic_slice_in_dim(skip_gain, me * piece, piece)[:, None]

    smem = pl.BlockSpec(memory_space=pltpu.SMEM)
    f32 = jnp.float32
    out = pl.pallas_call(
        local_kernel,
        out_shape=jax.ShapeDtypeStruct((blocks, piece, rows), jnp.bfloat16),
        in_specs=[smem, smem] + [vmem] * 9,
        out_specs=vmem,
        scratch_shapes=[
            pltpu.VMEM((blocks + 1, piece, rows), f32),
            pltpu.VMEM((blocks, piece, rows), f32),
            pltpu.VMEM((blocks, piece, rows), f32),
            pltpu.VMEM((2 * half * piece, 2 * rows), f32),
            pltpu.VMEM((half * piece, 2 * rows), f32),
        ],
    )(first, last, gathered, kern, gain, twist, untwist, c_hi, c_lo, s_hi, s_lo)

    everything = lax.all_gather(out, "ctx", axis=0)
    returned = lax.dynamic_index_in_dim(everything, me, axis=1, keepdims=False)
    return jnp.swapaxes(returned.reshape(chans, rows), 0, 1)


def solution(mesh):
    placed = (
        P(("groups", "ctx"), "ch"),
        P(("groups", "ctx"), "ch"),
        P(("groups", "ctx"), "ch"),
        P(None, None, "ch"),
        P("ctx", "ch"),
        P("ch"),
    )
    return jax.shard_map(
        body, mesh=mesh, in_specs=placed, out_specs=P(("groups", "ctx"), "ch"), check_vma=False
    )
```

```python
import math

import ml_dtypes
import numpy as np

import jax
import jax.numpy as jnp
from jax import lax
from jax.experimental import pallas as pl
from jax.experimental.pallas import tpu as pltpu
from jax.sharding import PartitionSpec as P

full_precision = lax.Precision.HIGHEST


def split_table(table):
    high = table.astype(ml_dtypes.bfloat16)
    low = (table - high.astype(np.float64)).astype(ml_dtypes.bfloat16)
    return jnp.asarray(high), jnp.asarray(low)


def kernel_tables(blocks, rows):
    total = 2 * blocks * rows
    half = blocks + 1
    k2 = np.arange(half)
    d = np.arange(blocks)
    r = np.arange(rows)
    clean = lambda a: np.where(np.abs(a) < 1e-12, 0.0, a)
    block_angle = 2.0 * np.pi * np.outer(k2, d) / (2 * blocks)
    first = clean(np.concatenate([np.cos(block_angle), -np.sin(block_angle)], axis=0))
    twist_angle = -2.0 * np.pi * np.outer(k2, r) / total
    twist = np.stack([np.cos(twist_angle), np.sin(twist_angle)])[:, :, None, :]
    untwist = np.stack([np.cos(twist_angle), -np.sin(twist_angle)])[:, :, None, :] / total
    row_angle = 2.0 * np.pi * np.outer(r, r) / rows
    weight = np.full(half, 2.0)
    weight[0] = 1.0
    weight[-1] = 1.0
    last_angle = 2.0 * np.pi * np.outer(d, k2) / (2 * blocks)
    last = clean(np.concatenate([weight * np.cos(last_angle), -weight * np.sin(last_angle)], axis=1))
    as_f32 = lambda a: jnp.asarray(a.astype(np.float32))
    return ((as_f32(first), as_f32(last), as_f32(twist), as_f32(untwist))
            + split_table(np.cos(row_angle)) + split_table(np.sin(row_angle)))


def scaled(terms):
    total = None
    for array, constant in terms:
        if array is None or constant == 0.0:
            continue
        if constant == 1.0:
            term = array
        elif constant == -1.0:
            term = -array
        else:
            term = constant * array
        total = term if total is None else total + term
    return total


def unit(angle):
    c, s = math.cos(angle), math.sin(angle)
    snap = lambda v: 0.0 if abs(v) < 1e-12 else (1.0 if abs(v - 1) < 1e-12 else (-1.0 if abs(v + 1) < 1e-12 else v))
    return snap(c), snap(s)


def fft(values, sign):
    count = len(values)
    if count == 1:
        return values
    even = fft(values[0::2], sign)
    odd = fft(values[1::2], sign)
    out = [None] * count
    for k in range(count // 2):
        c, s = unit(sign * 2.0 * math.pi * k / count)
        o_re, o_im = odd[k]
        t_re = scaled([(o_re, c), (o_im, -s)])
        t_im = scaled([(o_re, s), (o_im, c)])
        e_re, e_im = even[k]
        out[k] = (scaled([(e_re, 1.0), (t_re, 1.0)]), scaled([(e_im, 1.0), (t_im, 1.0)]))
        out[k + count // 2] = (scaled([(e_re, 1.0), (t_re, -1.0)]), scaled([(e_im, 1.0), (t_im, -1.0)]))
    return out


def halves(a):
    high = a.astype(jnp.bfloat16)
    return high, (a - high.astype(jnp.float32)).astype(jnp.bfloat16)


def times(parts, high_ref, low_ref):
    high, low = parts
    table = high_ref[...]
    out = jnp.dot(high, table, preferred_element_type=jnp.float32)
    out = out + jnp.dot(low, table, preferred_element_type=jnp.float32)
    return out + jnp.dot(high, low_ref[...], preferred_element_type=jnp.float32)


def local_kernel(first, last, sig, kern, gain, twist, untwist, c_hi, c_lo, s_hi, s_lo, out,
                 ext, g_s, o_s, a_all, a_h):
    blocks, piece, rows = out.shape
    half = blocks + 1
    taps = kern.shape[1]
    tile = min(piece, 8)
    unrolled = blocks <= 16
    f32 = jnp.float32
    lane = lax.broadcasted_iota(jnp.int32, (blocks, piece, rows), 2)

    def conv(stream, weights):
        x = sig[:, stream].astype(f32)
        total = kern[weights, 0] * x
        for lag in range(1, taps):
            rolled = pltpu.roll(x, lag, 2)
            before = jnp.concatenate([jnp.zeros_like(rolled[:1]), rolled[:-1]], axis=0)
            earlier = jnp.where(lane < lag, before, rolled)
            total = total + kern[weights, lag] * earlier
        return total

    g_s[...] = conv(0, 0) * conv(1, 2)
    o_s[...] = conv(2, 1)

    def load_block(which, d, at):
        if which == 0:
            return g_s[d, at, :]
        return sig[d, 3, at, :].astype(f32)

    for tile_index in range(piece // tile):
        at = pl.ds(tile_index * tile, tile)
        for which in range(2):
            base = which * half * piece
            if unrolled:
                xs = [(load_block(which, d, at), None) for d in range(blocks)]
                spectrum = fft(xs + [(None, None)] * blocks, -1.0)
                for k in range(half):
                    c, s = twist[0, k], twist[1, k]
                    re, im = spectrum[k]
                    if im is None:
                        turned = (re * c, re * s)
                    elif re is None:
                        turned = (-(im * s), im * c)
                    else:
                        turned = (re * c - im * s, re * s + im * c)
                    for part in range(2):
                        a_all[pl.ds(base + k * piece + tile_index * tile, tile), pl.ds(part * rows, rows)] = (
                            turned[part])
            else:
                for k in range(half):
                    for part in range(2):
                        a_all[pl.ds(base + k * piece + tile_index * tile, tile), pl.ds(part * rows, rows)] = (
                            jnp.zeros((tile, rows), f32))

                def step(d, carry):
                    xd = load_block(which, d, at)
                    for k in range(half):
                        for part in range(2):
                            where = (pl.ds(base + k * piece + tile_index * tile, tile), pl.ds(part * rows, rows))
                            a_all[where] = a_all[where] + first[part * half + k, d] * xd
                    return carry

                lax.fori_loop(0, blocks, step, 0)

    for which in range(0 if unrolled else 2):
        for k in range(half):
            at_rows = pl.ds(which * half * piece + k * piece, piece)
            re = a_all[at_rows, pl.ds(0, rows)]
            im = a_all[at_rows, pl.ds(rows, rows)]
            t_re = twist[0, k]
            t_im = twist[1, k]
            a_all[at_rows, pl.ds(0, rows)] = re * t_re - im * t_im
            a_all[at_rows, pl.ds(rows, rows)] = re * t_im + im * t_re
    re = halves(a_all[:, pl.ds(0, rows)])
    im = halves(a_all[:, pl.ds(rows, rows)])
    x_re = times(re, c_hi, c_lo) + times(im, s_hi, s_lo)
    x_im = times(im, c_hi, c_lo) - times(re, s_hi, s_lo)
    count = half * piece
    gr, gi = x_re[:count], x_im[:count]
    hr, hi = x_re[count:], x_im[count:]
    q_re = halves(gr * hr - gi * hi)
    q_im = halves(gr * hi + gi * hr)
    y_re = times(q_re, c_hi, c_lo) - times(q_im, s_hi, s_lo)
    y_im = times(q_re, s_hi, s_lo) + times(q_im, c_hi, c_lo)
    def untwisted(k, at_tile):
        lo = k * piece + at_tile * tile
        yr = y_re[lo:lo + tile]
        yi = y_im[lo:lo + tile]
        u_re = untwist[0, k]
        u_im = untwist[1, k]
        return yr * u_re - yi * u_im, yr * u_im + yi * u_re

    if not unrolled:
        for k in range(half):
            at_rows = pl.ds(k * piece, piece)
            yr = y_re[k * piece:(k + 1) * piece]
            yi = y_im[k * piece:(k + 1) * piece]
            a_h[at_rows, pl.ds(0, rows)] = yr * untwist[0, k] - yi * untwist[1, k]
            a_h[at_rows, pl.ds(rows, rows)] = yr * untwist[1, k] + yi * untwist[0, k]

    for tile_index in range(piece // tile):
        at = pl.ds(tile_index * tile, tile)
        scale = gain[at]

        def finish(d, us):
            acc = None
            for k in range(half):
                for part in range(2):
                    term = last[d, part * half + k] * us(k, part)
                    acc = term if acc is None else acc + term
            gated = g_s[d, at, :]
            out[d, at, :] = (o_s[d, at, :] * (acc + scale * gated)).astype(out.dtype)

        if unrolled:
            held = [untwisted(k, tile_index) for k in range(half)]
            full = held + [(re, -im) for re, im in reversed(held[1:blocks])]
            signal = fft(full, 1.0)
            for d in range(blocks):
                gated = g_s[d, at, :]
                out[d, at, :] = (o_s[d, at, :] * (signal[d][0] + scale * gated)).astype(out.dtype)
        else:
            def step(d, carry):
                finish(d, lambda k, part: a_h[
                    pl.ds(k * piece + tile_index * tile, tile), pl.ds(part * rows, rows)])
                return carry

            lax.fori_loop(0, blocks, step, 0)


def to_blocks_kernel(*refs):
    *streams, out, held = refs
    blocks, _, piece, rows = out.shape
    chans = held.shape[0]
    eye = (lax.broadcasted_iota(jnp.int32, (chans, chans), 0)
           == lax.broadcasted_iota(jnp.int32, (chans, chans), 1)).astype(jnp.bfloat16)
    for index, stream in enumerate(streams):
        held[...] = lax.dot_general(eye, stream[...], (((1,), (1,)), ((), ())),
                                    preferred_element_type=jnp.float32)
        for j in range(blocks):
            out[j, index] = held[pl.ds(j * piece, piece), :].astype(out.dtype)


def body(gate_stream, outer_stream, value_stream, short_weight, long_filter, skip_gain):
    rows, chans = gate_stream.shape
    blocks = lax.axis_size("ctx")
    piece = chans // blocks
    half = blocks + 1
    me = lax.axis_index("ctx")
    first, last, twist, untwist, c_hi, c_lo, s_hi, s_lo = kernel_tables(blocks, rows)

    vmem = pl.BlockSpec(memory_space=pltpu.VMEM)
    steps = 2
    step_rows = rows // steps
    stacked = pl.pallas_call(
        to_blocks_kernel,
        out_shape=jax.ShapeDtypeStruct((blocks, 4, piece, rows), jnp.bfloat16),
        grid=(steps,),
        in_specs=[pl.BlockSpec((step_rows, chans), lambda i: (i, 0))] * 4,
        out_specs=pl.BlockSpec((blocks, 4, piece, step_rows), lambda i: (0, 0, 0, i)),
        scratch_shapes=[pltpu.VMEM((chans, step_rows), jnp.float32)],
    )(gate_stream, value_stream, outer_stream, long_filter)
    gathered = lax.all_to_all(stacked, "ctx", 0, 0)

    kern = lax.dynamic_slice_in_dim(short_weight, me * piece, piece, axis=2).astype(jnp.float32)
    kern = kern[..., None]
    gain = lax.dynamic_slice_in_dim(skip_gain, me * piece, piece)[:, None]

    smem = pl.BlockSpec(memory_space=pltpu.SMEM)
    f32 = jnp.float32
    out = pl.pallas_call(
        local_kernel,
        out_shape=jax.ShapeDtypeStruct((blocks, piece, rows), jnp.bfloat16),
        in_specs=[smem, smem] + [vmem] * 9,
        out_specs=vmem,
        scratch_shapes=[
            pltpu.VMEM((blocks + 1, piece, rows), f32),
            pltpu.VMEM((blocks, piece, rows), f32),
            pltpu.VMEM((blocks, piece, rows), f32),
            pltpu.VMEM((2 * half * piece, 2 * rows), f32),
            pltpu.VMEM((half * piece, 2 * rows), f32),
        ],
    )(first, last, gathered, kern, gain, twist, untwist, c_hi, c_lo, s_hi, s_lo)

    returned = lax.all_to_all(out, "ctx", 0, 0)
    return jnp.swapaxes(returned.reshape(chans, rows), 0, 1)


def solution(mesh):
    placed = (
        P(("groups", "ctx"), "ch"),
        P(("groups", "ctx"), "ch"),
        P(("groups", "ctx"), "ch"),
        P(None, None, "ch"),
        P("ctx", "ch"),
        P("ch"),
    )
    return jax.shard_map(
        body, mesh=mesh, in_specs=placed, out_specs=P(("groups", "ctx"), "ch"), check_vma=False
    )
```

```python
import math

import ml_dtypes
import numpy as np

import jax
import jax.numpy as jnp
from jax import lax
from jax.experimental import pallas as pl
from jax.experimental.pallas import tpu as pltpu
from jax.sharding import PartitionSpec as P

full_precision = lax.Precision.HIGHEST


def split_table(table):
    high = table.astype(ml_dtypes.bfloat16)
    low = (table - high.astype(np.float64)).astype(ml_dtypes.bfloat16)
    return jnp.asarray(high), jnp.asarray(low)


def kernel_tables(blocks, rows):
    total = 2 * blocks * rows
    half = blocks + 1
    k2 = np.arange(half)
    d = np.arange(blocks)
    r = np.arange(rows)
    clean = lambda a: np.where(np.abs(a) < 1e-12, 0.0, a)
    block_angle = 2.0 * np.pi * np.outer(k2, d) / (2 * blocks)
    first = clean(np.concatenate([np.cos(block_angle), -np.sin(block_angle)], axis=0))
    twist_angle = -2.0 * np.pi * np.outer(k2, r) / total
    twist = np.stack([np.cos(twist_angle), np.sin(twist_angle)])[:, :, None, :]
    untwist = np.stack([np.cos(twist_angle), -np.sin(twist_angle)])[:, :, None, :] / total
    row_angle = 2.0 * np.pi * np.outer(r, r) / rows
    weight = np.full(half, 2.0)
    weight[0] = 1.0
    weight[-1] = 1.0
    last_angle = 2.0 * np.pi * np.outer(d, k2) / (2 * blocks)
    last = clean(np.concatenate([weight * np.cos(last_angle), -weight * np.sin(last_angle)], axis=1))
    as_f32 = lambda a: jnp.asarray(a.astype(np.float32))
    return ((as_f32(first), as_f32(last), as_f32(twist), as_f32(untwist))
            + split_table(np.cos(row_angle)) + split_table(np.sin(row_angle)))


def scaled(terms):
    total = None
    for array, constant in terms:
        if array is None or constant == 0.0:
            continue
        if constant == 1.0:
            term = array
        elif constant == -1.0:
            term = -array
        else:
            term = constant * array
        total = term if total is None else total + term
    return total


def unit(angle):
    c, s = math.cos(angle), math.sin(angle)
    snap = lambda v: 0.0 if abs(v) < 1e-12 else (1.0 if abs(v - 1) < 1e-12 else (-1.0 if abs(v + 1) < 1e-12 else v))
    return snap(c), snap(s)


def fft(values, sign):
    count = len(values)
    if count == 1:
        return values
    even = fft(values[0::2], sign)
    odd = fft(values[1::2], sign)
    out = [None] * count
    for k in range(count // 2):
        c, s = unit(sign * 2.0 * math.pi * k / count)
        o_re, o_im = odd[k]
        t_re = scaled([(o_re, c), (o_im, -s)])
        t_im = scaled([(o_re, s), (o_im, c)])
        e_re, e_im = even[k]
        out[k] = (scaled([(e_re, 1.0), (t_re, 1.0)]), scaled([(e_im, 1.0), (t_im, 1.0)]))
        out[k + count // 2] = (scaled([(e_re, 1.0), (t_re, -1.0)]), scaled([(e_im, 1.0), (t_im, -1.0)]))
    return out


def halves(a):
    high = a.astype(jnp.bfloat16)
    return high, (a - high.astype(jnp.float32)).astype(jnp.bfloat16)


def times(parts, high_ref, low_ref):
    high, low = parts
    table = high_ref[...]
    out = jnp.dot(high, table, preferred_element_type=jnp.float32)
    out = out + jnp.dot(low, table, preferred_element_type=jnp.float32)
    return out + jnp.dot(high, low_ref[...], preferred_element_type=jnp.float32)


def local_kernel(first, last, sig, kern, gain, twist, untwist, c_hi, c_lo, s_hi, s_lo, out,
                 ext, g_s, o_s, a_all, a_h):
    blocks, piece, rows = out.shape
    half = blocks + 1
    taps = kern.shape[1]
    tile = min(piece, 8)
    unrolled = blocks <= 16
    f32 = jnp.float32
    lane = lax.broadcasted_iota(jnp.int32, (blocks, piece, rows), 2)

    def conv(stream, weights):
        x = sig[:, stream].astype(f32)
        total = kern[weights, 0] * x
        for lag in range(1, taps):
            rolled = pltpu.roll(x, lag, 2)
            before = jnp.concatenate([jnp.zeros_like(rolled[:1]), rolled[:-1]], axis=0)
            earlier = jnp.where(lane < lag, before, rolled)
            total = total + kern[weights, lag] * earlier
        return total

    g_s[...] = conv(0, 0) * conv(1, 2)
    o_s[...] = conv(2, 1)

    def load_block(which, d, at):
        if which == 0:
            return g_s[d, at, :]
        return sig[d, 3, at, :].astype(f32)

    for tile_index in range(piece // tile):
        at = pl.ds(tile_index * tile, tile)
        for which in range(2):
            base = which * half * piece
            if unrolled:
                xs = [(load_block(which, d, at), None) for d in range(blocks)]
                spectrum = fft(xs + [(None, None)] * blocks, -1.0)
                for k in range(half):
                    c, s = twist[0, k], twist[1, k]
                    re, im = spectrum[k]
                    if im is None:
                        turned = (re * c, re * s)
                    elif re is None:
                        turned = (-(im * s), im * c)
                    else:
                        turned = (re * c - im * s, re * s + im * c)
                    for part in range(2):
                        a_all[pl.ds(base + k * piece + tile_index * tile, tile), pl.ds(part * rows, rows)] = (
                            turned[part])
            else:
                for k in range(half):
                    for part in range(2):
                        a_all[pl.ds(base + k * piece + tile_index * tile, tile), pl.ds(part * rows, rows)] = (
                            jnp.zeros((tile, rows), f32))

                def step(d, carry):
                    xd = load_block(which, d, at)
                    for k in range(half):
                        for part in range(2):
                            where = (pl.ds(base + k * piece + tile_index * tile, tile), pl.ds(part * rows, rows))
                            a_all[where] = a_all[where] + first[part * half + k, d] * xd
                    return carry

                lax.fori_loop(0, blocks, step, 0)

    for which in range(0 if unrolled else 2):
        for k in range(half):
            at_rows = pl.ds(which * half * piece + k * piece, piece)
            re = a_all[at_rows, pl.ds(0, rows)]
            im = a_all[at_rows, pl.ds(rows, rows)]
            t_re = twist[0, k]
            t_im = twist[1, k]
            a_all[at_rows, pl.ds(0, rows)] = re * t_re - im * t_im
            a_all[at_rows, pl.ds(rows, rows)] = re * t_im + im * t_re
    re = halves(a_all[:, pl.ds(0, rows)])
    im = halves(a_all[:, pl.ds(rows, rows)])
    x_re = times(re, c_hi, c_lo) + times(im, s_hi, s_lo)
    x_im = times(im, c_hi, c_lo) - times(re, s_hi, s_lo)
    count = half * piece
    gr, gi = x_re[:count], x_im[:count]
    hr, hi = x_re[count:], x_im[count:]
    q_re = halves(gr * hr - gi * hi)
    q_im = halves(gr * hi + gi * hr)
    y_re = times(q_re, c_hi, c_lo) - times(q_im, s_hi, s_lo)
    y_im = times(q_re, s_hi, s_lo) + times(q_im, c_hi, c_lo)
    def untwisted(k, at_tile):
        lo = k * piece + at_tile * tile
        yr = y_re[lo:lo + tile]
        yi = y_im[lo:lo + tile]
        u_re = untwist[0, k]
        u_im = untwist[1, k]
        return yr * u_re - yi * u_im, yr * u_im + yi * u_re

    if not unrolled:
        for k in range(half):
            at_rows = pl.ds(k * piece, piece)
            yr = y_re[k * piece:(k + 1) * piece]
            yi = y_im[k * piece:(k + 1) * piece]
            a_h[at_rows, pl.ds(0, rows)] = yr * untwist[0, k] - yi * untwist[1, k]
            a_h[at_rows, pl.ds(rows, rows)] = yr * untwist[1, k] + yi * untwist[0, k]

    for tile_index in range(piece // tile):
        at = pl.ds(tile_index * tile, tile)
        scale = gain[at]

        def finish(d, us):
            acc = None
            for k in range(half):
                for part in range(2):
                    term = last[d, part * half + k] * us(k, part)
                    acc = term if acc is None else acc + term
            gated = g_s[d, at, :]
            out[d, at, :] = (o_s[d, at, :] * (acc + scale * gated)).astype(out.dtype)

        if unrolled:
            held = [untwisted(k, tile_index) for k in range(half)]
            full = held + [(re, -im) for re, im in reversed(held[1:blocks])]
            signal = fft(full, 1.0)
            for d in range(blocks):
                gated = g_s[d, at, :]
                out[d, at, :] = (o_s[d, at, :] * (signal[d][0] + scale * gated)).astype(out.dtype)
        else:
            def step(d, carry):
                finish(d, lambda k, part: a_h[
                    pl.ds(k * piece + tile_index * tile, tile), pl.ds(part * rows, rows)])
                return carry

            lax.fori_loop(0, blocks, step, 0)


def to_blocks_kernel(*refs):
    *streams, out, held = refs
    blocks, _, piece, rows = out.shape
    chans = held.shape[0]
    eye = (lax.broadcasted_iota(jnp.int32, (chans, chans), 0)
           == lax.broadcasted_iota(jnp.int32, (chans, chans), 1)).astype(jnp.bfloat16)
    for index, stream in enumerate(streams):
        held[...] = lax.dot_general(eye, stream[...], (((1,), (1,)), ((), ())),
                                    preferred_element_type=jnp.float32)
        for j in range(blocks):
            out[j, index] = held[pl.ds(j * piece, piece), :].astype(out.dtype)


def body(gate_stream, outer_stream, value_stream, short_weight, long_filter, skip_gain):
    rows, chans = gate_stream.shape
    blocks = lax.axis_size("ctx")
    piece = chans // blocks
    half = blocks + 1
    me = lax.axis_index("ctx")
    first, last, twist, untwist, c_hi, c_lo, s_hi, s_lo = kernel_tables(blocks, rows)

    vmem = pl.BlockSpec(memory_space=pltpu.VMEM)
    stacked = pl.pallas_call(
        to_blocks_kernel,
        out_shape=jax.ShapeDtypeStruct((blocks, 4, piece, rows), jnp.bfloat16),
        in_specs=[vmem] * 4,
        out_specs=vmem,
        scratch_shapes=[pltpu.VMEM((chans, rows), jnp.float32)],
    )(gate_stream, value_stream, outer_stream, long_filter)
    flat = stacked.reshape(blocks * 4 * piece, rows)
    gathered = lax.all_to_all(flat, "ctx", 0, 0, tiled=True).reshape(stacked.shape)

    kern = lax.dynamic_slice_in_dim(short_weight, me * piece, piece, axis=2).astype(jnp.float32)
    kern = kern[..., None]
    gain = lax.dynamic_slice_in_dim(skip_gain, me * piece, piece)[:, None]

    smem = pl.BlockSpec(memory_space=pltpu.SMEM)
    f32 = jnp.float32
    out = pl.pallas_call(
        local_kernel,
        out_shape=jax.ShapeDtypeStruct((blocks, piece, rows), jnp.bfloat16),
        in_specs=[smem, smem] + [vmem] * 9,
        out_specs=vmem,
        scratch_shapes=[
            pltpu.VMEM((blocks + 1, piece, rows), f32),
            pltpu.VMEM((blocks, piece, rows), f32),
            pltpu.VMEM((blocks, piece, rows), f32),
            pltpu.VMEM((2 * half * piece, 2 * rows), f32),
            pltpu.VMEM((half * piece, 2 * rows), f32),
        ],
    )(first, last, gathered, kern, gain, twist, untwist, c_hi, c_lo, s_hi, s_lo)

    returned = lax.all_to_all(out.reshape(chans, rows), "ctx", 0, 0, tiled=True)
    return jnp.swapaxes(returned, 0, 1)


def solution(mesh):
    placed = (
        P(("groups", "ctx"), "ch"),
        P(("groups", "ctx"), "ch"),
        P(("groups", "ctx"), "ch"),
        P(None, None, "ch"),
        P("ctx", "ch"),
        P("ch"),
    )
    return jax.shard_map(
        body, mesh=mesh, in_specs=placed, out_specs=P(("groups", "ctx"), "ch"), check_vma=False
    )
```

```python
import math

import ml_dtypes
import numpy as np

import jax
import jax.numpy as jnp
from jax import lax
from jax.experimental import pallas as pl
from jax.experimental.pallas import tpu as pltpu
from jax.sharding import PartitionSpec as P

full_precision = lax.Precision.HIGHEST


def split_table(table):
    high = table.astype(ml_dtypes.bfloat16)
    low = (table - high.astype(np.float64)).astype(ml_dtypes.bfloat16)
    return jnp.asarray(high), jnp.asarray(low)


def kernel_tables(blocks, rows):
    total = 2 * blocks * rows
    half = blocks + 1
    k2 = np.arange(half)
    d = np.arange(blocks)
    r = np.arange(rows)
    clean = lambda a: np.where(np.abs(a) < 1e-12, 0.0, a)
    block_angle = 2.0 * np.pi * np.outer(k2, d) / (2 * blocks)
    first = clean(np.concatenate([np.cos(block_angle), -np.sin(block_angle)], axis=0))
    twist_angle = -2.0 * np.pi * np.outer(k2, r) / total
    twist = np.stack([np.cos(twist_angle), np.sin(twist_angle)])[:, :, None, :]
    untwist = np.stack([np.cos(twist_angle), -np.sin(twist_angle)])[:, :, None, :] / total
    row_angle = 2.0 * np.pi * np.outer(r, r) / rows
    weight = np.full(half, 2.0)
    weight[0] = 1.0
    weight[-1] = 1.0
    last_angle = 2.0 * np.pi * np.outer(d, k2) / (2 * blocks)
    last = clean(np.concatenate([weight * np.cos(last_angle), -weight * np.sin(last_angle)], axis=1))
    as_f32 = lambda a: jnp.asarray(a.astype(np.float32))
    c_hi, c_lo = split_table(np.cos(row_angle))
    s_hi, s_lo = split_table(np.sin(row_angle))
    turns = as_f32(np.concatenate([twist, untwist], axis=0))
    return as_f32(first), as_f32(last), turns, jnp.stack([c_hi, c_lo, s_hi, s_lo])


def scaled(terms):
    total = None
    for array, constant in terms:
        if array is None or constant == 0.0:
            continue
        if constant == 1.0:
            term = array
        elif constant == -1.0:
            term = -array
        else:
            term = constant * array
        total = term if total is None else total + term
    return total


def unit(angle):
    c, s = math.cos(angle), math.sin(angle)
    snap = lambda v: 0.0 if abs(v) < 1e-12 else (1.0 if abs(v - 1) < 1e-12 else (-1.0 if abs(v + 1) < 1e-12 else v))
    return snap(c), snap(s)


def fft(values, sign):
    count = len(values)
    if count == 1:
        return values
    even = fft(values[0::2], sign)
    odd = fft(values[1::2], sign)
    out = [None] * count
    for k in range(count // 2):
        c, s = unit(sign * 2.0 * math.pi * k / count)
        o_re, o_im = odd[k]
        t_re = scaled([(o_re, c), (o_im, -s)])
        t_im = scaled([(o_re, s), (o_im, c)])
        e_re, e_im = even[k]
        out[k] = (scaled([(e_re, 1.0), (t_re, 1.0)]), scaled([(e_im, 1.0), (t_im, 1.0)]))
        out[k + count // 2] = (scaled([(e_re, 1.0), (t_re, -1.0)]), scaled([(e_im, 1.0), (t_im, -1.0)]))
    return out


def halves(a):
    high = a.astype(jnp.bfloat16)
    return high, (a - high.astype(jnp.float32)).astype(jnp.bfloat16)


def times(parts, high_ref, low_ref):
    high, low = parts
    table = high_ref[...]
    out = jnp.dot(high, table, preferred_element_type=jnp.float32)
    out = out + jnp.dot(low, table, preferred_element_type=jnp.float32)
    return out + jnp.dot(high, low_ref[...], preferred_element_type=jnp.float32)


def local_kernel(first, last, sig, kern, gain, turns, tabs, out,
                 ext, g_s, o_s, a_all, a_h):
    twist, untwist = turns.at[0:2], turns.at[2:4]
    c_hi, c_lo, s_hi, s_lo = (tabs.at[i] for i in range(4))
    blocks, piece, rows = out.shape
    half = blocks + 1
    taps = kern.shape[1]
    tile = min(piece, 8)
    unrolled = blocks <= 16
    f32 = jnp.float32
    lane = lax.broadcasted_iota(jnp.int32, (blocks, piece, rows), 2)

    def conv(stream, weights):
        x = sig[:, stream].astype(f32)
        total = kern[weights, 0] * x
        for lag in range(1, taps):
            rolled = pltpu.roll(x, lag, 2)
            before = jnp.concatenate([jnp.zeros_like(rolled[:1]), rolled[:-1]], axis=0)
            earlier = jnp.where(lane < lag, before, rolled)
            total = total + kern[weights, lag] * earlier
        return total

    g_s[...] = conv(0, 0) * conv(1, 2)
    o_s[...] = conv(2, 1)

    def load_block(which, d, at):
        if which == 0:
            return g_s[d, at, :]
        return sig[d, 3, at, :].astype(f32)

    for tile_index in range(piece // tile):
        at = pl.ds(tile_index * tile, tile)
        for which in range(2):
            base = which * half * piece
            if unrolled:
                xs = [(load_block(which, d, at), None) for d in range(blocks)]
                spectrum = fft(xs + [(None, None)] * blocks, -1.0)
                for k in range(half):
                    c, s = twist[0, k], twist[1, k]
                    re, im = spectrum[k]
                    if im is None:
                        turned = (re * c, re * s)
                    elif re is None:
                        turned = (-(im * s), im * c)
                    else:
                        turned = (re * c - im * s, re * s + im * c)
                    for part in range(2):
                        a_all[pl.ds(base + k * piece + tile_index * tile, tile), pl.ds(part * rows, rows)] = (
                            turned[part])
            else:
                for k in range(half):
                    for part in range(2):
                        a_all[pl.ds(base + k * piece + tile_index * tile, tile), pl.ds(part * rows, rows)] = (
                            jnp.zeros((tile, rows), f32))

                def step(d, carry):
                    xd = load_block(which, d, at)
                    for k in range(half):
                        for part in range(2):
                            where = (pl.ds(base + k * piece + tile_index * tile, tile), pl.ds(part * rows, rows))
                            a_all[where] = a_all[where] + first[part * half + k, d] * xd
                    return carry

                lax.fori_loop(0, blocks, step, 0)

    for which in range(0 if unrolled else 2):
        for k in range(half):
            at_rows = pl.ds(which * half * piece + k * piece, piece)
            re = a_all[at_rows, pl.ds(0, rows)]
            im = a_all[at_rows, pl.ds(rows, rows)]
            t_re = twist[0, k]
            t_im = twist[1, k]
            a_all[at_rows, pl.ds(0, rows)] = re * t_re - im * t_im
            a_all[at_rows, pl.ds(rows, rows)] = re * t_im + im * t_re
    re = halves(a_all[:, pl.ds(0, rows)])
    im = halves(a_all[:, pl.ds(rows, rows)])
    x_re = times(re, c_hi, c_lo) + times(im, s_hi, s_lo)
    x_im = times(im, c_hi, c_lo) - times(re, s_hi, s_lo)
    count = half * piece
    gr, gi = x_re[:count], x_im[:count]
    hr, hi = x_re[count:], x_im[count:]
    q_re = halves(gr * hr - gi * hi)
    q_im = halves(gr * hi + gi * hr)
    y_re = times(q_re, c_hi, c_lo) - times(q_im, s_hi, s_lo)
    y_im = times(q_re, s_hi, s_lo) + times(q_im, c_hi, c_lo)
    def untwisted(k, at_tile):
        lo = k * piece + at_tile * tile
        yr = y_re[lo:lo + tile]
        yi = y_im[lo:lo + tile]
        u_re = untwist[0, k]
        u_im = untwist[1, k]
        return yr * u_re - yi * u_im, yr * u_im + yi * u_re

    if not unrolled:
        for k in range(half):
            at_rows = pl.ds(k * piece, piece)
            yr = y_re[k * piece:(k + 1) * piece]
            yi = y_im[k * piece:(k + 1) * piece]
            a_h[at_rows, pl.ds(0, rows)] = yr * untwist[0, k] - yi * untwist[1, k]
            a_h[at_rows, pl.ds(rows, rows)] = yr * untwist[1, k] + yi * untwist[0, k]

    for tile_index in range(piece // tile):
        at = pl.ds(tile_index * tile, tile)
        scale = gain[at]

        def finish(d, us):
            acc = None
            for k in range(half):
                for part in range(2):
                    term = last[d, part * half + k] * us(k, part)
                    acc = term if acc is None else acc + term
            gated = g_s[d, at, :]
            out[d, at, :] = (o_s[d, at, :] * (acc + scale * gated)).astype(out.dtype)

        if unrolled:
            held = [untwisted(k, tile_index) for k in range(half)]
            full = held + [(re, -im) for re, im in reversed(held[1:blocks])]
            signal = fft(full, 1.0)
            for d in range(blocks):
                gated = g_s[d, at, :]
                out[d, at, :] = (o_s[d, at, :] * (signal[d][0] + scale * gated)).astype(out.dtype)
        else:
            def step(d, carry):
                finish(d, lambda k, part: a_h[
                    pl.ds(k * piece + tile_index * tile, tile), pl.ds(part * rows, rows)])
                return carry

            lax.fori_loop(0, blocks, step, 0)


def to_blocks_kernel(*refs):
    *streams, out, held = refs
    blocks, _, piece, rows = out.shape
    chans = held.shape[0]
    eye = (lax.broadcasted_iota(jnp.int32, (chans, chans), 0)
           == lax.broadcasted_iota(jnp.int32, (chans, chans), 1)).astype(jnp.bfloat16)
    for index, stream in enumerate(streams):
        held[...] = lax.dot_general(eye, stream[...], (((1,), (1,)), ((), ())),
                                    preferred_element_type=jnp.float32)
        for j in range(blocks):
            out[j, index] = held[pl.ds(j * piece, piece), :].astype(out.dtype)


def body(gate_stream, outer_stream, value_stream, short_weight, long_filter, skip_gain):
    rows, chans = gate_stream.shape
    blocks = lax.axis_size("ctx")
    piece = chans // blocks
    half = blocks + 1
    me = lax.axis_index("ctx")
    first, last, turns, tabs = kernel_tables(blocks, rows)

    vmem = pl.BlockSpec(memory_space=pltpu.VMEM)
    stacked = pl.pallas_call(
        to_blocks_kernel,
        out_shape=jax.ShapeDtypeStruct((blocks, 4, piece, rows), jnp.bfloat16),
        in_specs=[vmem] * 4,
        out_specs=vmem,
        scratch_shapes=[pltpu.VMEM((chans, rows), jnp.float32)],
    )(gate_stream, value_stream, outer_stream, long_filter)
    gathered = lax.all_to_all(stacked, "ctx", 0, 0)

    kern = lax.dynamic_slice_in_dim(short_weight, me * piece, piece, axis=2).astype(jnp.float32)
    kern = kern[..., None]
    gain = lax.dynamic_slice_in_dim(skip_gain, me * piece, piece)[:, None]

    smem = pl.BlockSpec(memory_space=pltpu.SMEM)
    f32 = jnp.float32
    out = pl.pallas_call(
        local_kernel,
        out_shape=jax.ShapeDtypeStruct((blocks, piece, rows), jnp.bfloat16),
        in_specs=[smem, smem] + [vmem] * 5,
        out_specs=vmem,
        scratch_shapes=[
            pltpu.VMEM((blocks + 1, piece, rows), f32),
            pltpu.VMEM((blocks, piece, rows), f32),
            pltpu.VMEM((blocks, piece, rows), f32),
            pltpu.VMEM((2 * half * piece, 2 * rows), f32),
            pltpu.VMEM((half * piece, 2 * rows), f32),
        ],
    )(first, last, gathered, kern, gain, turns, tabs)

    returned = lax.all_to_all(out, "ctx", 0, 0)
    return jnp.swapaxes(returned.reshape(chans, rows), 0, 1)


def solution(mesh):
    placed = (
        P(("groups", "ctx"), "ch"),
        P(("groups", "ctx"), "ch"),
        P(("groups", "ctx"), "ch"),
        P(None, None, "ch"),
        P("ctx", "ch"),
        P("ch"),
    )
    return jax.shard_map(
        body, mesh=mesh, in_specs=placed, out_specs=P(("groups", "ctx"), "ch"), check_vma=False
    )
```

```python
import math

import ml_dtypes
import numpy as np

import jax
import jax.numpy as jnp
from jax import lax
from jax.experimental import pallas as pl
from jax.experimental.pallas import tpu as pltpu
from jax.sharding import PartitionSpec as P

full_precision = lax.Precision.HIGHEST


def split_table(table):
    high = table.astype(ml_dtypes.bfloat16)
    low = (table - high.astype(np.float64)).astype(ml_dtypes.bfloat16)
    return jnp.asarray(high), jnp.asarray(low)


def kernel_tables(blocks, rows):
    total = 2 * blocks * rows
    half = blocks + 1
    k2 = np.arange(half)
    d = np.arange(blocks)
    r = np.arange(rows)
    clean = lambda a: np.where(np.abs(a) < 1e-12, 0.0, a)
    block_angle = 2.0 * np.pi * np.outer(k2, d) / (2 * blocks)
    first = clean(np.concatenate([np.cos(block_angle), -np.sin(block_angle)], axis=0))
    twist_angle = -2.0 * np.pi * np.outer(k2, r) / total
    twist = np.stack([np.cos(twist_angle), np.sin(twist_angle)])[:, :, None, :]
    untwist = np.stack([np.cos(twist_angle), -np.sin(twist_angle)])[:, :, None, :] / total
    row_angle = 2.0 * np.pi * np.outer(r, r) / rows
    weight = np.full(half, 2.0)
    weight[0] = 1.0
    weight[-1] = 1.0
    last_angle = 2.0 * np.pi * np.outer(d, k2) / (2 * blocks)
    last = clean(np.concatenate([weight * np.cos(last_angle), -weight * np.sin(last_angle)], axis=1))
    as_f32 = lambda a: jnp.asarray(a.astype(np.float32))
    return ((as_f32(first), as_f32(last), as_f32(twist), as_f32(untwist))
            + split_table(np.cos(row_angle)) + split_table(np.sin(row_angle)))


def scaled(terms):
    total = None
    for array, constant in terms:
        if array is None or constant == 0.0:
            continue
        if constant == 1.0:
            term = array
        elif constant == -1.0:
            term = -array
        else:
            term = constant * array
        total = term if total is None else total + term
    return total


def unit(angle):
    c, s = math.cos(angle), math.sin(angle)
    snap = lambda v: 0.0 if abs(v) < 1e-12 else (1.0 if abs(v - 1) < 1e-12 else (-1.0 if abs(v + 1) < 1e-12 else v))
    return snap(c), snap(s)


def fft(values, sign):
    count = len(values)
    if count == 1:
        return values
    even = fft(values[0::2], sign)
    odd = fft(values[1::2], sign)
    out = [None] * count
    for k in range(count // 2):
        c, s = unit(sign * 2.0 * math.pi * k / count)
        o_re, o_im = odd[k]
        t_re = scaled([(o_re, c), (o_im, -s)])
        t_im = scaled([(o_re, s), (o_im, c)])
        e_re, e_im = even[k]
        out[k] = (scaled([(e_re, 1.0), (t_re, 1.0)]), scaled([(e_im, 1.0), (t_im, 1.0)]))
        out[k + count // 2] = (scaled([(e_re, 1.0), (t_re, -1.0)]), scaled([(e_im, 1.0), (t_im, -1.0)]))
    return out


def halves(a):
    high = a.astype(jnp.bfloat16)
    return high, (a - high.astype(jnp.float32)).astype(jnp.bfloat16)


def times(parts, high_ref, low_ref):
    high, low = parts
    table = high_ref[...]
    out = jnp.dot(high, table, preferred_element_type=jnp.float32)
    out = out + jnp.dot(low, table, preferred_element_type=jnp.float32)
    return out + jnp.dot(high, low_ref[...], preferred_element_type=jnp.float32)


def local_kernel(first, last, sig, kern, gain, twist, untwist, c_hi, c_lo, s_hi, s_lo, out,
                 ext, g_s, o_s, a_all, a_h):
    blocks, piece, rows = out.shape
    half = blocks + 1
    taps = kern.shape[1]
    tile = min(piece, 8)
    unrolled = blocks <= 16
    f32 = jnp.float32
    lane = lax.broadcasted_iota(jnp.int32, (blocks, piece, rows), 2)

    def conv(stream, weights):
        x = sig[:, stream].astype(f32)
        total = kern[weights, 0] * x
        for lag in range(1, taps):
            rolled = pltpu.roll(x, lag, 2)
            before = jnp.concatenate([jnp.zeros_like(rolled[:1]), rolled[:-1]], axis=0)
            earlier = jnp.where(lane < lag, before, rolled)
            total = total + kern[weights, lag] * earlier
        return total

    g_s[...] = conv(0, 0) * conv(1, 2)
    o_s[...] = conv(2, 1)

    def load_block(which, d, at):
        if which == 0:
            return g_s[d, at, :]
        return sig[d, 3, at, :].astype(f32)

    for tile_index in range(piece // tile):
        at = pl.ds(tile_index * tile, tile)
        for which in range(2):
            base = which * half * piece
            if unrolled:
                xs = [(load_block(which, d, at), None) for d in range(blocks)]
                spectrum = fft(xs + [(None, None)] * blocks, -1.0)
                for k in range(half):
                    c, s = twist[0, k], twist[1, k]
                    re, im = spectrum[k]
                    if im is None:
                        turned = (re * c, re * s)
                    elif re is None:
                        turned = (-(im * s), im * c)
                    else:
                        turned = (re * c - im * s, re * s + im * c)
                    for part in range(2):
                        a_all[pl.ds(base + k * piece + tile_index * tile, tile), pl.ds(part * rows, rows)] = (
                            turned[part])
            else:
                for k in range(half):
                    for part in range(2):
                        a_all[pl.ds(base + k * piece + tile_index * tile, tile), pl.ds(part * rows, rows)] = (
                            jnp.zeros((tile, rows), f32))

                def step(d, carry):
                    xd = load_block(which, d, at)
                    for k in range(half):
                        for part in range(2):
                            where = (pl.ds(base + k * piece + tile_index * tile, tile), pl.ds(part * rows, rows))
                            a_all[where] = a_all[where] + first[part * half + k, d] * xd
                    return carry

                lax.fori_loop(0, blocks, step, 0)

    for which in range(0 if unrolled else 2):
        for k in range(half):
            at_rows = pl.ds(which * half * piece + k * piece, piece)
            re = a_all[at_rows, pl.ds(0, rows)]
            im = a_all[at_rows, pl.ds(rows, rows)]
            t_re = twist[0, k]
            t_im = twist[1, k]
            a_all[at_rows, pl.ds(0, rows)] = re * t_re - im * t_im
            a_all[at_rows, pl.ds(rows, rows)] = re * t_im + im * t_re
    re = halves(a_all[:, pl.ds(0, rows)])
    im = halves(a_all[:, pl.ds(rows, rows)])
    x_re = times(re, c_hi, c_lo) + times(im, s_hi, s_lo)
    x_im = times(im, c_hi, c_lo) - times(re, s_hi, s_lo)
    count = half * piece
    gr, gi = x_re[:count], x_im[:count]
    hr, hi = x_re[count:], x_im[count:]
    q_re = halves(gr * hr - gi * hi)
    q_im = halves(gr * hi + gi * hr)
    y_re = times(q_re, c_hi, c_lo) - times(q_im, s_hi, s_lo)
    y_im = times(q_re, s_hi, s_lo) + times(q_im, c_hi, c_lo)
    def untwisted(k, at_tile):
        lo = k * piece + at_tile * tile
        yr = y_re[lo:lo + tile]
        yi = y_im[lo:lo + tile]
        u_re = untwist[0, k]
        u_im = untwist[1, k]
        return yr * u_re - yi * u_im, yr * u_im + yi * u_re

    if not unrolled:
        for k in range(half):
            at_rows = pl.ds(k * piece, piece)
            yr = y_re[k * piece:(k + 1) * piece]
            yi = y_im[k * piece:(k + 1) * piece]
            a_h[at_rows, pl.ds(0, rows)] = yr * untwist[0, k] - yi * untwist[1, k]
            a_h[at_rows, pl.ds(rows, rows)] = yr * untwist[1, k] + yi * untwist[0, k]

    for tile_index in range(piece // tile):
        at = pl.ds(tile_index * tile, tile)
        scale = gain[at]

        def finish(d, us):
            acc = None
            for k in range(half):
                for part in range(2):
                    term = last[d, part * half + k] * us(k, part)
                    acc = term if acc is None else acc + term
            gated = g_s[d, at, :]
            out[d, at, :] = (o_s[d, at, :] * (acc + scale * gated)).astype(out.dtype)

        if unrolled:
            held = [untwisted(k, tile_index) for k in range(half)]
            full = held + [(re, -im) for re, im in reversed(held[1:blocks])]
            signal = fft(full, 1.0)
            for d in range(blocks):
                gated = g_s[d, at, :]
                out[d, at, :] = (o_s[d, at, :] * (signal[d][0] + scale * gated)).astype(out.dtype)
        else:
            def step(d, carry):
                finish(d, lambda k, part: a_h[
                    pl.ds(k * piece + tile_index * tile, tile), pl.ds(part * rows, rows)])
                return carry

            lax.fori_loop(0, blocks, step, 0)


def to_blocks_kernel(*refs):
    *streams, out, held = refs
    blocks, _, piece, rows = out.shape
    chans = held.shape[0]
    eye = (lax.broadcasted_iota(jnp.int32, (chans, chans), 0)
           == lax.broadcasted_iota(jnp.int32, (chans, chans), 1)).astype(jnp.bfloat16)
    for index, stream in enumerate(streams):
        held[...] = lax.dot_general(eye, stream[...], (((1,), (1,)), ((), ())),
                                    preferred_element_type=jnp.float32)
        for j in range(blocks):
            out[j, index] = held[pl.ds(j * piece, piece), :].astype(out.dtype)


def body(gate_stream, outer_stream, value_stream, short_weight, long_filter, skip_gain):
    rows, chans = gate_stream.shape
    blocks = lax.axis_size("ctx")
    piece = chans // blocks
    half = blocks + 1
    me = lax.axis_index("ctx")
    first, last, twist, untwist, c_hi, c_lo, s_hi, s_lo = kernel_tables(blocks, rows)

    vmem = pl.BlockSpec(memory_space=pltpu.VMEM)
    stacked = pl.pallas_call(
        to_blocks_kernel,
        out_shape=jax.ShapeDtypeStruct((blocks, 4, piece, rows), jnp.bfloat16),
        in_specs=[vmem] * 4,
        out_specs=vmem,
        scratch_shapes=[pltpu.VMEM((chans, rows), jnp.float32)],
    )(gate_stream, value_stream, outer_stream, long_filter)
    gathered = lax.all_to_all(stacked, "ctx", 0, 0)

    kern = lax.dynamic_slice_in_dim(short_weight, me * piece, piece, axis=2).astype(jnp.float32)
    kern = kern[..., None]
    gain = lax.dynamic_slice_in_dim(skip_gain, me * piece, piece)[:, None]

    smem = pl.BlockSpec(memory_space=pltpu.SMEM)
    f32 = jnp.float32
    out = pl.pallas_call(
        local_kernel,
        out_shape=jax.ShapeDtypeStruct((blocks, piece, rows), jnp.bfloat16),
        in_specs=[smem, smem] + [vmem] * 9,
        out_specs=vmem,
        scratch_shapes=[
            pltpu.VMEM((blocks + 1, piece, rows), f32),
            pltpu.VMEM((blocks, piece, rows), f32),
            pltpu.VMEM((blocks, piece, rows), f32),
            pltpu.VMEM((2 * half * piece, 2 * rows), f32),
            pltpu.VMEM((half * piece, 2 * rows), f32),
        ],
        compiler_params=pltpu.CompilerParams(vmem_limit_bytes=24 * 1024 * 1024),
    )(first, last, gathered, kern, gain, twist, untwist, c_hi, c_lo, s_hi, s_lo)

    returned = lax.all_to_all(out, "ctx", 0, 0)
    return jnp.swapaxes(returned.reshape(chans, rows), 0, 1)


def solution(mesh):
    placed = (
        P(("groups", "ctx"), "ch"),
        P(("groups", "ctx"), "ch"),
        P(("groups", "ctx"), "ch"),
        P(None, None, "ch"),
        P("ctx", "ch"),
        P("ch"),
    )
    return jax.shard_map(
        body, mesh=mesh, in_specs=placed, out_specs=P(("groups", "ctx"), "ch"), check_vma=False
    )
```

```python
import math

import ml_dtypes
import numpy as np

import jax
import jax.numpy as jnp
from jax import lax
from jax.experimental import pallas as pl
from jax.experimental.pallas import tpu as pltpu
from jax.sharding import PartitionSpec as P

full_precision = lax.Precision.HIGHEST


def split_table(table):
    high = table.astype(ml_dtypes.bfloat16)
    low = (table - high.astype(np.float64)).astype(ml_dtypes.bfloat16)
    return jnp.asarray(high), jnp.asarray(low)


def kernel_tables(blocks, rows):
    total = 2 * blocks * rows
    half = blocks + 1
    k2 = np.arange(half)
    d = np.arange(blocks)
    r = np.arange(rows)
    clean = lambda a: np.where(np.abs(a) < 1e-12, 0.0, a)
    block_angle = 2.0 * np.pi * np.outer(k2, d) / (2 * blocks)
    first = clean(np.concatenate([np.cos(block_angle), -np.sin(block_angle)], axis=0))
    twist_angle = -2.0 * np.pi * np.outer(k2, r) / total
    twist = np.stack([np.cos(twist_angle), np.sin(twist_angle)])[:, :, None, :]
    untwist = np.stack([np.cos(twist_angle), -np.sin(twist_angle)])[:, :, None, :] / total
    row_angle = 2.0 * np.pi * np.outer(r, r) / rows
    weight = np.full(half, 2.0)
    weight[0] = 1.0
    weight[-1] = 1.0
    last_angle = 2.0 * np.pi * np.outer(d, k2) / (2 * blocks)
    last = clean(np.concatenate([weight * np.cos(last_angle), -weight * np.sin(last_angle)], axis=1))
    as_f32 = lambda a: jnp.asarray(a.astype(np.float32))
    return ((as_f32(first), as_f32(last), as_f32(twist), as_f32(untwist))
            + split_table(np.cos(row_angle)) + split_table(np.sin(row_angle)))


def scaled(terms):
    total = None
    for array, constant in terms:
        if array is None or constant == 0.0:
            continue
        if constant == 1.0:
            term = array
        elif constant == -1.0:
            term = -array
        else:
            term = constant * array
        total = term if total is None else total + term
    return total


def unit(angle):
    c, s = math.cos(angle), math.sin(angle)
    snap = lambda v: 0.0 if abs(v) < 1e-12 else (1.0 if abs(v - 1) < 1e-12 else (-1.0 if abs(v + 1) < 1e-12 else v))
    return snap(c), snap(s)


def fft(values, sign):
    count = len(values)
    if count == 1:
        return values
    even = fft(values[0::2], sign)
    odd = fft(values[1::2], sign)
    out = [None] * count
    for k in range(count // 2):
        c, s = unit(sign * 2.0 * math.pi * k / count)
        o_re, o_im = odd[k]
        t_re = scaled([(o_re, c), (o_im, -s)])
        t_im = scaled([(o_re, s), (o_im, c)])
        e_re, e_im = even[k]
        out[k] = (scaled([(e_re, 1.0), (t_re, 1.0)]), scaled([(e_im, 1.0), (t_im, 1.0)]))
        out[k + count // 2] = (scaled([(e_re, 1.0), (t_re, -1.0)]), scaled([(e_im, 1.0), (t_im, -1.0)]))
    return out


def halves(a):
    high = a.astype(jnp.bfloat16)
    return high, (a - high.astype(jnp.float32)).astype(jnp.bfloat16)


def times(parts, high_ref, low_ref):
    high, low = parts
    table = high_ref[...]
    out = jnp.dot(high, table, preferred_element_type=jnp.float32)
    out = out + jnp.dot(low, table, preferred_element_type=jnp.float32)
    return out + jnp.dot(high, low_ref[...], preferred_element_type=jnp.float32)


def local_kernel(first, last, sig, kern, gain, twist, untwist, c_hi, c_lo, s_hi, s_lo, out,
                 ext, g_s, o_s, a_all, a_h):
    blocks, piece, rows = out.shape
    half = blocks + 1
    taps = kern.shape[1]
    tile = min(piece, 8)
    unrolled = blocks <= 16
    f32 = jnp.float32
    lane = lax.broadcasted_iota(jnp.int32, (blocks, piece, rows), 2)

    def conv(stream, weights):
        x = sig[:, stream].astype(f32)
        total = kern[weights, 0] * x
        for lag in range(1, taps):
            rolled = pltpu.roll(x, lag, 2)
            before = jnp.concatenate([jnp.zeros_like(rolled[:1]), rolled[:-1]], axis=0)
            earlier = jnp.where(lane < lag, before, rolled)
            total = total + kern[weights, lag] * earlier
        return total

    g_s[...] = conv(0, 0) * conv(1, 2)
    o_s[...] = conv(2, 1)

    def load_block(which, d, at):
        if which == 0:
            return g_s[d, at, :]
        return sig[d, 3, at, :].astype(f32)

    for tile_index in range(piece // tile):
        at = pl.ds(tile_index * tile, tile)
        for which in range(2):
            base = which * half * piece
            if unrolled:
                xs = [(load_block(which, d, at), None) for d in range(blocks)]
                spectrum = fft(xs + [(None, None)] * blocks, -1.0)
                for k in range(half):
                    c, s = twist[0, k], twist[1, k]
                    re, im = spectrum[k]
                    if im is None:
                        turned = (re * c, re * s)
                    elif re is None:
                        turned = (-(im * s), im * c)
                    else:
                        turned = (re * c - im * s, re * s + im * c)
                    for part in range(2):
                        a_all[pl.ds(base + k * piece + tile_index * tile, tile), pl.ds(part * rows, rows)] = (
                            turned[part])
            else:
                for k in range(half):
                    for part in range(2):
                        a_all[pl.ds(base + k * piece + tile_index * tile, tile), pl.ds(part * rows, rows)] = (
                            jnp.zeros((tile, rows), f32))

                def step(d, carry):
                    xd = load_block(which, d, at)
                    for k in range(half):
                        for part in range(2):
                            where = (pl.ds(base + k * piece + tile_index * tile, tile), pl.ds(part * rows, rows))
                            a_all[where] = a_all[where] + first[part * half + k, d] * xd
                    return carry

                lax.fori_loop(0, blocks, step, 0)

    for which in range(0 if unrolled else 2):
        for k in range(half):
            at_rows = pl.ds(which * half * piece + k * piece, piece)
            re = a_all[at_rows, pl.ds(0, rows)]
            im = a_all[at_rows, pl.ds(rows, rows)]
            t_re = twist[0, k]
            t_im = twist[1, k]
            a_all[at_rows, pl.ds(0, rows)] = re * t_re - im * t_im
            a_all[at_rows, pl.ds(rows, rows)] = re * t_im + im * t_re
    re = halves(a_all[:, pl.ds(0, rows)])
    im = halves(a_all[:, pl.ds(rows, rows)])
    x_re = times(re, c_hi, c_lo) + times(im, s_hi, s_lo)
    x_im = times(im, c_hi, c_lo) - times(re, s_hi, s_lo)
    count = half * piece
    gr, gi = x_re[:count], x_im[:count]
    hr, hi = x_re[count:], x_im[count:]
    q_re = halves(gr * hr - gi * hi)
    q_im = halves(gr * hi + gi * hr)
    y_re = times(q_re, c_hi, c_lo) - times(q_im, s_hi, s_lo)
    y_im = times(q_re, s_hi, s_lo) + times(q_im, c_hi, c_lo)
    def untwisted(k, at_tile):
        lo = k * piece + at_tile * tile
        yr = y_re[lo:lo + tile]
        yi = y_im[lo:lo + tile]
        u_re = untwist[0, k]
        u_im = untwist[1, k]
        return yr * u_re - yi * u_im, yr * u_im + yi * u_re

    if not unrolled:
        for k in range(half):
            at_rows = pl.ds(k * piece, piece)
            yr = y_re[k * piece:(k + 1) * piece]
            yi = y_im[k * piece:(k + 1) * piece]
            a_h[at_rows, pl.ds(0, rows)] = yr * untwist[0, k] - yi * untwist[1, k]
            a_h[at_rows, pl.ds(rows, rows)] = yr * untwist[1, k] + yi * untwist[0, k]

    for tile_index in range(piece // tile):
        at = pl.ds(tile_index * tile, tile)
        scale = gain[at]

        def finish(d, us):
            acc = None
            for k in range(half):
                for part in range(2):
                    term = last[d, part * half + k] * us(k, part)
                    acc = term if acc is None else acc + term
            gated = g_s[d, at, :]
            out[d, at, :] = (o_s[d, at, :] * (acc + scale * gated)).astype(out.dtype)

        if unrolled:
            held = [untwisted(k, tile_index) for k in range(half)]
            full = held + [(re, -im) for re, im in reversed(held[1:blocks])]
            signal = fft(full, 1.0)
            for d in range(blocks):
                gated = g_s[d, at, :]
                out[d, at, :] = (o_s[d, at, :] * (signal[d][0] + scale * gated)).astype(out.dtype)
        else:
            def step(d, carry):
                finish(d, lambda k, part: a_h[
                    pl.ds(k * piece + tile_index * tile, tile), pl.ds(part * rows, rows)])
                return carry

            lax.fori_loop(0, blocks, step, 0)


def to_blocks_kernel(*refs):
    *streams, out, held = refs
    blocks, _, piece, rows = out.shape
    chans = held.shape[0]
    eye = (lax.broadcasted_iota(jnp.int32, (chans, chans), 0)
           == lax.broadcasted_iota(jnp.int32, (chans, chans), 1)).astype(jnp.bfloat16)
    for index, stream in enumerate(streams):
        held[...] = lax.dot_general(eye, stream[...], (((1,), (1,)), ((), ())),
                                    preferred_element_type=jnp.float32)
        for j in range(blocks):
            out[j, index] = held[pl.ds(j * piece, piece), :].astype(out.dtype)


def body(gate_stream, outer_stream, value_stream, short_weight, long_filter, skip_gain):
    rows, chans = gate_stream.shape
    blocks = lax.axis_size("ctx")
    piece = chans // blocks
    half = blocks + 1
    me = lax.axis_index("ctx")
    first, last, twist, untwist, c_hi, c_lo, s_hi, s_lo = kernel_tables(blocks, rows)

    vmem = pl.BlockSpec(memory_space=pltpu.VMEM)
    stacked = pl.pallas_call(
        to_blocks_kernel,
        out_shape=jax.ShapeDtypeStruct((blocks, 4, piece, rows), jnp.bfloat16),
        in_specs=[vmem] * 4,
        out_specs=vmem,
        scratch_shapes=[pltpu.VMEM((chans, rows), jnp.float32)],
        compiler_params=pltpu.CompilerParams(vmem_limit_bytes=16 * 1024 * 1024),
    )(gate_stream, value_stream, outer_stream, long_filter)
    gathered = lax.all_to_all(stacked, "ctx", 0, 0)

    kern = lax.dynamic_slice_in_dim(short_weight, me * piece, piece, axis=2).astype(jnp.float32)
    kern = kern[..., None]
    gain = lax.dynamic_slice_in_dim(skip_gain, me * piece, piece)[:, None]

    smem = pl.BlockSpec(memory_space=pltpu.SMEM)
    f32 = jnp.float32
    out = pl.pallas_call(
        local_kernel,
        out_shape=jax.ShapeDtypeStruct((blocks, piece, rows), jnp.bfloat16),
        in_specs=[smem, smem] + [vmem] * 9,
        out_specs=vmem,
        scratch_shapes=[
            pltpu.VMEM((blocks + 1, piece, rows), f32),
            pltpu.VMEM((blocks, piece, rows), f32),
            pltpu.VMEM((blocks, piece, rows), f32),
            pltpu.VMEM((2 * half * piece, 2 * rows), f32),
            pltpu.VMEM((half * piece, 2 * rows), f32),
        ],
        compiler_params=pltpu.CompilerParams(vmem_limit_bytes=24 * 1024 * 1024),
    )(first, last, gathered, kern, gain, twist, untwist, c_hi, c_lo, s_hi, s_lo)

    returned = lax.all_to_all(out, "ctx", 0, 0)
    return jnp.swapaxes(returned.reshape(chans, rows), 0, 1)


def solution(mesh):
    placed = (
        P(("groups", "ctx"), "ch"),
        P(("groups", "ctx"), "ch"),
        P(("groups", "ctx"), "ch"),
        P(None, None, "ch"),
        P("ctx", "ch"),
        P("ch"),
    )
    return jax.shard_map(
        body, mesh=mesh, in_specs=placed, out_specs=P(("groups", "ctx"), "ch"), check_vma=False
    )
```

```python
import math

import ml_dtypes
import numpy as np

import jax
import jax.numpy as jnp
from jax import lax
from jax.experimental import pallas as pl
from jax.experimental.pallas import tpu as pltpu
from jax.sharding import PartitionSpec as P

full_precision = lax.Precision.HIGHEST


def split_table(table):
    high = table.astype(ml_dtypes.bfloat16)
    low = (table - high.astype(np.float64)).astype(ml_dtypes.bfloat16)
    return jnp.asarray(high), jnp.asarray(low)


def kernel_tables(blocks, rows):
    total = 2 * blocks * rows
    half = blocks + 1
    k2 = np.arange(half)
    d = np.arange(blocks)
    r = np.arange(rows)
    clean = lambda a: np.where(np.abs(a) < 1e-12, 0.0, a)
    block_angle = 2.0 * np.pi * np.outer(k2, d) / (2 * blocks)
    first = clean(np.concatenate([np.cos(block_angle), -np.sin(block_angle)], axis=0))
    twist_angle = -2.0 * np.pi * np.outer(k2, r) / total
    twist = np.stack([np.cos(twist_angle), np.sin(twist_angle)])[:, :, None, :]
    untwist = np.stack([np.cos(twist_angle), -np.sin(twist_angle)])[:, :, None, :] / total
    row_angle = 2.0 * np.pi * np.outer(r, r) / rows
    weight = np.full(half, 2.0)
    weight[0] = 1.0
    weight[-1] = 1.0
    last_angle = 2.0 * np.pi * np.outer(d, k2) / (2 * blocks)
    last = clean(np.concatenate([weight * np.cos(last_angle), -weight * np.sin(last_angle)], axis=1))
    as_f32 = lambda a: jnp.asarray(a.astype(np.float32))
    return ((as_f32(first), as_f32(last), as_f32(twist), as_f32(untwist))
            + split_table(np.cos(row_angle)) + split_table(np.sin(row_angle)))


def scaled(terms):
    total = None
    for array, constant in terms:
        if array is None or constant == 0.0:
            continue
        if constant == 1.0:
            term = array
        elif constant == -1.0:
            term = -array
        else:
            term = constant * array
        total = term if total is None else total + term
    return total


def unit(angle):
    c, s = math.cos(angle), math.sin(angle)
    snap = lambda v: 0.0 if abs(v) < 1e-12 else (1.0 if abs(v - 1) < 1e-12 else (-1.0 if abs(v + 1) < 1e-12 else v))
    return snap(c), snap(s)


def fft(values, sign):
    count = len(values)
    if count == 1:
        return values
    even = fft(values[0::2], sign)
    odd = fft(values[1::2], sign)
    out = [None] * count
    for k in range(count // 2):
        c, s = unit(sign * 2.0 * math.pi * k / count)
        o_re, o_im = odd[k]
        t_re = scaled([(o_re, c), (o_im, -s)])
        t_im = scaled([(o_re, s), (o_im, c)])
        e_re, e_im = even[k]
        out[k] = (scaled([(e_re, 1.0), (t_re, 1.0)]), scaled([(e_im, 1.0), (t_im, 1.0)]))
        out[k + count // 2] = (scaled([(e_re, 1.0), (t_re, -1.0)]), scaled([(e_im, 1.0), (t_im, -1.0)]))
    return out


def halves(a):
    high = a.astype(jnp.bfloat16)
    return high, (a - high.astype(jnp.float32)).astype(jnp.bfloat16)


def times(parts, high_ref, low_ref):
    high, low = parts
    table = high_ref[...]
    out = jnp.dot(high, table, preferred_element_type=jnp.float32)
    out = out + jnp.dot(low, table, preferred_element_type=jnp.float32)
    return out + jnp.dot(high, low_ref[...], preferred_element_type=jnp.float32)


def local_kernel(first, last, sig, kern, gain, twist, untwist, c_hi, c_lo, s_hi, s_lo, out,
                 ext, g_s, o_s, a_all, a_h):
    blocks, piece, rows = out.shape
    half = blocks + 1
    taps = kern.shape[1]
    tile = min(piece, 8)
    unrolled = blocks <= 16
    f32 = jnp.float32
    lane = lax.broadcasted_iota(jnp.int32, (blocks, piece, rows), 2)

    def conv(stream, weights):
        x = sig[:, stream].astype(f32)
        total = kern[weights, 0] * x
        for lag in range(1, taps):
            rolled = pltpu.roll(x, lag, 2)
            before = jnp.concatenate([jnp.zeros_like(rolled[:1]), rolled[:-1]], axis=0)
            earlier = jnp.where(lane < lag, before, rolled)
            total = total + kern[weights, lag] * earlier
        return total

    g_s[...] = conv(0, 0) * conv(1, 2)
    o_s[...] = conv(2, 1)

    def load_block(which, d, at):
        if which == 0:
            return g_s[d, at, :]
        return sig[d, 3, at, :].astype(f32)

    for tile_index in range(piece // tile):
        at = pl.ds(tile_index * tile, tile)
        for which in range(2):
            base = which * half * piece
            if unrolled:
                xs = [(load_block(which, d, at), None) for d in range(blocks)]
                spectrum = fft(xs + [(None, None)] * blocks, -1.0)
                for k in range(half):
                    c, s = twist[0, k], twist[1, k]
                    re, im = spectrum[k]
                    if im is None:
                        turned = (re * c, re * s)
                    elif re is None:
                        turned = (-(im * s), im * c)
                    else:
                        turned = (re * c - im * s, re * s + im * c)
                    for part in range(2):
                        a_all[pl.ds(base + k * piece + tile_index * tile, tile), pl.ds(part * rows, rows)] = (
                            turned[part])
            else:
                for k in range(half):
                    for part in range(2):
                        a_all[pl.ds(base + k * piece + tile_index * tile, tile), pl.ds(part * rows, rows)] = (
                            jnp.zeros((tile, rows), f32))

                def step(d, carry):
                    xd = load_block(which, d, at)
                    for k in range(half):
                        for part in range(2):
                            where = (pl.ds(base + k * piece + tile_index * tile, tile), pl.ds(part * rows, rows))
                            a_all[where] = a_all[where] + first[part * half + k, d] * xd
                    return carry

                lax.fori_loop(0, blocks, step, 0)

    for which in range(0 if unrolled else 2):
        for k in range(half):
            at_rows = pl.ds(which * half * piece + k * piece, piece)
            re = a_all[at_rows, pl.ds(0, rows)]
            im = a_all[at_rows, pl.ds(rows, rows)]
            t_re = twist[0, k]
            t_im = twist[1, k]
            a_all[at_rows, pl.ds(0, rows)] = re * t_re - im * t_im
            a_all[at_rows, pl.ds(rows, rows)] = re * t_im + im * t_re
    re = halves(a_all[:, pl.ds(0, rows)])
    im = halves(a_all[:, pl.ds(rows, rows)])
    x_re = times(re, c_hi, c_lo) + times(im, s_hi, s_lo)
    x_im = times(im, c_hi, c_lo) - times(re, s_hi, s_lo)
    count = half * piece
    gr, gi = x_re[:count], x_im[:count]
    hr, hi = x_re[count:], x_im[count:]
    q_re = halves(gr * hr - gi * hi)
    q_im = halves(gr * hi + gi * hr)
    y_re = times(q_re, c_hi, c_lo) - times(q_im, s_hi, s_lo)
    y_im = times(q_re, s_hi, s_lo) + times(q_im, c_hi, c_lo)
    def untwisted(k, at_tile):
        lo = k * piece + at_tile * tile
        yr = y_re[lo:lo + tile]
        yi = y_im[lo:lo + tile]
        u_re = untwist[0, k]
        u_im = untwist[1, k]
        return yr * u_re - yi * u_im, yr * u_im + yi * u_re

    if not unrolled:
        for k in range(half):
            at_rows = pl.ds(k * piece, piece)
            yr = y_re[k * piece:(k + 1) * piece]
            yi = y_im[k * piece:(k + 1) * piece]
            a_h[at_rows, pl.ds(0, rows)] = yr * untwist[0, k] - yi * untwist[1, k]
            a_h[at_rows, pl.ds(rows, rows)] = yr * untwist[1, k] + yi * untwist[0, k]

    for tile_index in range(piece // tile):
        at = pl.ds(tile_index * tile, tile)
        scale = gain[at]

        def finish(d, us):
            acc = None
            for k in range(half):
                for part in range(2):
                    term = last[d, part * half + k] * us(k, part)
                    acc = term if acc is None else acc + term
            gated = g_s[d, at, :]
            out[d, at, :] = (o_s[d, at, :] * (acc + scale * gated)).astype(out.dtype)

        if unrolled:
            held = [untwisted(k, tile_index) for k in range(half)]
            full = held + [(re, -im) for re, im in reversed(held[1:blocks])]
            signal = fft(full, 1.0)
            for d in range(blocks):
                gated = g_s[d, at, :]
                out[d, at, :] = (o_s[d, at, :] * (signal[d][0] + scale * gated)).astype(out.dtype)
        else:
            def step(d, carry):
                finish(d, lambda k, part: a_h[
                    pl.ds(k * piece + tile_index * tile, tile), pl.ds(part * rows, rows)])
                return carry

            lax.fori_loop(0, blocks, step, 0)


def to_blocks_kernel(*refs):
    *streams, out, held = refs
    blocks, _, piece, rows = out.shape
    chans = held.shape[0]
    eye = (lax.broadcasted_iota(jnp.int32, (chans, chans), 0)
           == lax.broadcasted_iota(jnp.int32, (chans, chans), 1)).astype(jnp.bfloat16)
    for index, stream in enumerate(streams):
        held[...] = lax.dot_general(eye, stream[...], (((1,), (1,)), ((), ())),
                                    preferred_element_type=jnp.float32)
        for j in range(blocks):
            out[j, index] = held[pl.ds(j * piece, piece), :].astype(out.dtype)


def body(gate_stream, outer_stream, value_stream, short_weight, long_filter, skip_gain):
    rows, chans = gate_stream.shape
    blocks = lax.axis_size("ctx")
    piece = chans // blocks
    half = blocks + 1
    me = lax.axis_index("ctx")
    first, last, twist, untwist, c_hi, c_lo, s_hi, s_lo = kernel_tables(blocks, rows)

    vmem = pl.BlockSpec(memory_space=pltpu.VMEM)
    stacked = pl.pallas_call(
        to_blocks_kernel,
        out_shape=jax.ShapeDtypeStruct((blocks, 4, piece, rows), jnp.bfloat16),
        in_specs=[vmem] * 4,
        out_specs=vmem,
        scratch_shapes=[pltpu.VMEM((chans, rows), jnp.float32)],
    )(gate_stream, value_stream, outer_stream, long_filter)
    gathered = lax.all_to_all(stacked, "ctx", 0, 0)

    kern = lax.dynamic_slice_in_dim(short_weight, me * piece, piece, axis=2).astype(jnp.float32)
    kern = kern[..., None]
    gain = lax.dynamic_slice_in_dim(skip_gain, me * piece, piece)[:, None]

    smem = pl.BlockSpec(memory_space=pltpu.SMEM)
    f32 = jnp.float32
    out = pl.pallas_call(
        local_kernel,
        out_shape=jax.ShapeDtypeStruct((blocks, piece, rows), jnp.bfloat16),
        in_specs=[smem, smem] + [vmem] * 9,
        out_specs=vmem,
        scratch_shapes=[
            pltpu.VMEM((blocks + 1, piece, rows), f32),
            pltpu.VMEM((blocks, piece, rows), f32),
            pltpu.VMEM((blocks, piece, rows), f32),
            pltpu.VMEM((2 * half * piece, 2 * rows), f32),
            pltpu.VMEM((half * piece, 2 * rows), f32),
        ],
        compiler_params=pltpu.CompilerParams(vmem_limit_bytes=12 * 1024 * 1024),
    )(first, last, gathered, kern, gain, twist, untwist, c_hi, c_lo, s_hi, s_lo)

    returned = lax.all_to_all(out, "ctx", 0, 0)
    return jnp.swapaxes(returned.reshape(chans, rows), 0, 1)


def solution(mesh):
    placed = (
        P(("groups", "ctx"), "ch"),
        P(("groups", "ctx"), "ch"),
        P(("groups", "ctx"), "ch"),
        P(None, None, "ch"),
        P("ctx", "ch"),
        P("ch"),
    )
    return jax.shard_map(
        body, mesh=mesh, in_specs=placed, out_specs=P(("groups", "ctx"), "ch"), check_vma=False
    )
```

```python
import math

import ml_dtypes
import numpy as np

import jax
import jax.numpy as jnp
from jax import lax
from jax.experimental import pallas as pl
from jax.experimental.pallas import tpu as pltpu
from jax.sharding import PartitionSpec as P

full_precision = lax.Precision.HIGHEST


def split_table(table):
    high = table.astype(ml_dtypes.bfloat16)
    low = (table - high.astype(np.float64)).astype(ml_dtypes.bfloat16)
    return jnp.asarray(high), jnp.asarray(low)


def kernel_tables(blocks, rows):
    total = 2 * blocks * rows
    half = blocks + 1
    k2 = np.arange(half)
    d = np.arange(blocks)
    r = np.arange(rows)
    clean = lambda a: np.where(np.abs(a) < 1e-12, 0.0, a)
    block_angle = 2.0 * np.pi * np.outer(k2, d) / (2 * blocks)
    first = clean(np.concatenate([np.cos(block_angle), -np.sin(block_angle)], axis=0))
    twist_angle = -2.0 * np.pi * np.outer(k2, r) / total
    twist = np.stack([np.cos(twist_angle), np.sin(twist_angle)])[:, :, None, :]
    untwist = np.stack([np.cos(twist_angle), -np.sin(twist_angle)])[:, :, None, :] / total
    row_angle = 2.0 * np.pi * np.outer(r, r) / rows
    weight = np.full(half, 2.0)
    weight[0] = 1.0
    weight[-1] = 1.0
    last_angle = 2.0 * np.pi * np.outer(d, k2) / (2 * blocks)
    last = clean(np.concatenate([weight * np.cos(last_angle), -weight * np.sin(last_angle)], axis=1))
    as_f32 = lambda a: jnp.asarray(a.astype(np.float32))
    c_hi, c_lo = split_table(np.cos(row_angle))
    s_hi, s_lo = split_table(np.sin(row_angle))
    turns = as_f32(np.concatenate([twist, untwist], axis=0))
    return as_f32(first), as_f32(last), turns, jnp.stack([c_hi, c_lo, s_hi, s_lo])


def scaled(terms):
    total = None
    for array, constant in terms:
        if array is None or constant == 0.0:
            continue
        if constant == 1.0:
            term = array
        elif constant == -1.0:
            term = -array
        else:
            term = constant * array
        total = term if total is None else total + term
    return total


def unit(angle):
    c, s = math.cos(angle), math.sin(angle)
    snap = lambda v: 0.0 if abs(v) < 1e-12 else (1.0 if abs(v - 1) < 1e-12 else (-1.0 if abs(v + 1) < 1e-12 else v))
    return snap(c), snap(s)


def fft(values, sign):
    count = len(values)
    if count == 1:
        return values
    even = fft(values[0::2], sign)
    odd = fft(values[1::2], sign)
    out = [None] * count
    for k in range(count // 2):
        c, s = unit(sign * 2.0 * math.pi * k / count)
        o_re, o_im = odd[k]
        t_re = scaled([(o_re, c), (o_im, -s)])
        t_im = scaled([(o_re, s), (o_im, c)])
        e_re, e_im = even[k]
        out[k] = (scaled([(e_re, 1.0), (t_re, 1.0)]), scaled([(e_im, 1.0), (t_im, 1.0)]))
        out[k + count // 2] = (scaled([(e_re, 1.0), (t_re, -1.0)]), scaled([(e_im, 1.0), (t_im, -1.0)]))
    return out


def halves(a):
    high = a.astype(jnp.bfloat16)
    return high, (a - high.astype(jnp.float32)).astype(jnp.bfloat16)


def times(parts, high_ref, low_ref):
    high, low = parts
    table = high_ref[...]
    out = jnp.dot(high, table, preferred_element_type=jnp.float32)
    out = out + jnp.dot(low, table, preferred_element_type=jnp.float32)
    return out + jnp.dot(high, low_ref[...], preferred_element_type=jnp.float32)


def local_kernel(first, last, sig, kern, gain, turns, tabs, out,
                 ext, g_s, o_s, a_all, a_h):
    twist, untwist = turns.at[0:2], turns.at[2:4]
    c_hi, c_lo, s_hi, s_lo = (tabs.at[i] for i in range(4))
    blocks, piece, rows = out.shape
    half = blocks + 1
    taps = kern.shape[1]
    tile = min(piece, 8)
    unrolled = blocks <= 16
    f32 = jnp.float32
    lane = lax.broadcasted_iota(jnp.int32, (blocks, piece, rows), 2)

    def conv(stream, weights):
        x = sig[:, stream].astype(f32)
        total = kern[weights, 0] * x
        for lag in range(1, taps):
            rolled = pltpu.roll(x, lag, 2)
            before = jnp.concatenate([jnp.zeros_like(rolled[:1]), rolled[:-1]], axis=0)
            earlier = jnp.where(lane < lag, before, rolled)
            total = total + kern[weights, lag] * earlier
        return total

    g_s[...] = conv(0, 0) * conv(1, 2)
    o_s[...] = conv(2, 1)

    def load_block(which, d, at):
        if which == 0:
            return g_s[d, at, :]
        return sig[d, 3, at, :].astype(f32)

    for tile_index in range(piece // tile):
        at = pl.ds(tile_index * tile, tile)
        for which in range(2):
            base = which * half * piece
            if unrolled:
                xs = [(load_block(which, d, at), None) for d in range(blocks)]
                spectrum = fft(xs + [(None, None)] * blocks, -1.0)
                for k in range(half):
                    c, s = twist[0, k], twist[1, k]
                    re, im = spectrum[k]
                    if im is None:
                        turned = (re * c, re * s)
                    elif re is None:
                        turned = (-(im * s), im * c)
                    else:
                        turned = (re * c - im * s, re * s + im * c)
                    for part in range(2):
                        a_all[pl.ds(base + k * piece + tile_index * tile, tile), pl.ds(part * rows, rows)] = (
                            turned[part])
            else:
                for k in range(half):
                    for part in range(2):
                        a_all[pl.ds(base + k * piece + tile_index * tile, tile), pl.ds(part * rows, rows)] = (
                            jnp.zeros((tile, rows), f32))

                def step(d, carry):
                    xd = load_block(which, d, at)
                    for k in range(half):
                        for part in range(2):
                            where = (pl.ds(base + k * piece + tile_index * tile, tile), pl.ds(part * rows, rows))
                            a_all[where] = a_all[where] + first[part * half + k, d] * xd
                    return carry

                lax.fori_loop(0, blocks, step, 0)

    for which in range(0 if unrolled else 2):
        for k in range(half):
            at_rows = pl.ds(which * half * piece + k * piece, piece)
            re = a_all[at_rows, pl.ds(0, rows)]
            im = a_all[at_rows, pl.ds(rows, rows)]
            t_re = twist[0, k]
            t_im = twist[1, k]
            a_all[at_rows, pl.ds(0, rows)] = re * t_re - im * t_im
            a_all[at_rows, pl.ds(rows, rows)] = re * t_im + im * t_re
    re = halves(a_all[:, pl.ds(0, rows)])
    im = halves(a_all[:, pl.ds(rows, rows)])
    x_re = times(re, c_hi, c_lo) + times(im, s_hi, s_lo)
    x_im = times(im, c_hi, c_lo) - times(re, s_hi, s_lo)
    count = half * piece
    gr, gi = x_re[:count], x_im[:count]
    hr, hi = x_re[count:], x_im[count:]
    q_re = halves(gr * hr - gi * hi)
    q_im = halves(gr * hi + gi * hr)
    y_re = times(q_re, c_hi, c_lo) - times(q_im, s_hi, s_lo)
    y_im = times(q_re, s_hi, s_lo) + times(q_im, c_hi, c_lo)
    def untwisted(k, at_tile):
        lo = k * piece + at_tile * tile
        yr = y_re[lo:lo + tile]
        yi = y_im[lo:lo + tile]
        u_re = untwist[0, k]
        u_im = untwist[1, k]
        return yr * u_re - yi * u_im, yr * u_im + yi * u_re

    if not unrolled:
        for k in range(half):
            at_rows = pl.ds(k * piece, piece)
            yr = y_re[k * piece:(k + 1) * piece]
            yi = y_im[k * piece:(k + 1) * piece]
            a_h[at_rows, pl.ds(0, rows)] = yr * untwist[0, k] - yi * untwist[1, k]
            a_h[at_rows, pl.ds(rows, rows)] = yr * untwist[1, k] + yi * untwist[0, k]

    for tile_index in range(piece // tile):
        at = pl.ds(tile_index * tile, tile)
        scale = gain[at]

        def finish(d, us):
            acc = None
            for k in range(half):
                for part in range(2):
                    term = last[d, part * half + k] * us(k, part)
                    acc = term if acc is None else acc + term
            gated = g_s[d, at, :]
            out[d, at, :] = (o_s[d, at, :] * (acc + scale * gated)).astype(out.dtype)

        if unrolled:
            held = [untwisted(k, tile_index) for k in range(half)]
            full = held + [(re, -im) for re, im in reversed(held[1:blocks])]
            signal = fft(full, 1.0)
            for d in range(blocks):
                gated = g_s[d, at, :]
                out[d, at, :] = (o_s[d, at, :] * (signal[d][0] + scale * gated)).astype(out.dtype)
        else:
            def step(d, carry):
                finish(d, lambda k, part: a_h[
                    pl.ds(k * piece + tile_index * tile, tile), pl.ds(part * rows, rows)])
                return carry

            lax.fori_loop(0, blocks, step, 0)


def to_blocks_kernel(*refs):
    *streams, out, held = refs
    blocks, _, piece, rows = out.shape
    chans = held.shape[0]
    eye = (lax.broadcasted_iota(jnp.int32, (chans, chans), 0)
           == lax.broadcasted_iota(jnp.int32, (chans, chans), 1)).astype(jnp.bfloat16)
    for index, stream in enumerate(streams):
        held[...] = lax.dot_general(eye, stream[...], (((1,), (1,)), ((), ())),
                                    preferred_element_type=jnp.float32)
        for j in range(blocks):
            out[j, index] = held[pl.ds(j * piece, piece), :].astype(out.dtype)


def body(gate_stream, outer_stream, value_stream, short_weight, long_filter, skip_gain):
    rows, chans = gate_stream.shape
    blocks = lax.axis_size("ctx")
    piece = chans // blocks
    half = blocks + 1
    me = lax.axis_index("ctx")
    first, last, turns, tabs = kernel_tables(blocks, rows)

    vmem = pl.BlockSpec(memory_space=pltpu.VMEM)
    stacked = pl.pallas_call(
        to_blocks_kernel,
        out_shape=jax.ShapeDtypeStruct((blocks, 4, piece, rows), jnp.bfloat16),
        in_specs=[vmem] * 4,
        out_specs=vmem,
        scratch_shapes=[pltpu.VMEM((chans, rows), jnp.float32)],
    )(gate_stream, value_stream, outer_stream, long_filter)
    gathered = lax.all_to_all(stacked, "ctx", 0, 0)

    kern = lax.dynamic_slice_in_dim(short_weight, me * piece, piece, axis=2).astype(jnp.float32)
    kern = kern[..., None]
    gain = lax.dynamic_slice_in_dim(skip_gain, me * piece, piece)[:, None]

    smem = pl.BlockSpec(memory_space=pltpu.SMEM)
    f32 = jnp.float32
    out = pl.pallas_call(
        local_kernel,
        out_shape=jax.ShapeDtypeStruct((blocks, piece, rows), jnp.bfloat16),
        in_specs=[smem, smem] + [vmem] * 5,
        out_specs=vmem,
        scratch_shapes=[
            pltpu.VMEM((blocks + 1, piece, rows), f32),
            pltpu.VMEM((blocks, piece, rows), f32),
            pltpu.VMEM((blocks, piece, rows), f32),
            pltpu.VMEM((2 * half * piece, 2 * rows), f32),
            pltpu.VMEM((half * piece, 2 * rows), f32),
        ],
        compiler_params=pltpu.CompilerParams(vmem_limit_bytes=24 * 1024 * 1024),
    )(first, last, gathered, kern, gain, turns, tabs)

    returned = lax.all_to_all(out, "ctx", 0, 0)
    return jnp.swapaxes(returned.reshape(chans, rows), 0, 1)


def solution(mesh):
    placed = (
        P(("groups", "ctx"), "ch"),
        P(("groups", "ctx"), "ch"),
        P(("groups", "ctx"), "ch"),
        P(None, None, "ch"),
        P("ctx", "ch"),
        P("ch"),
    )
    return jax.shard_map(
        body, mesh=mesh, in_specs=placed, out_specs=P(("groups", "ctx"), "ch"), check_vma=False
    )
```
